32 devices in a mesh: grp: 2 (over x), seq: 16 (over z, y, core).
Axes of the slice: x: 2, y: 2, z: 4, core: 2. Of those that a mesh axis runs over, the one named last changes fastest.
Arguments:
- tile_embeds: bfloat16 [16384, 1536], P(('grp', 'seq')), parts along dimension 0, may hold values from -6 to 6
- tile_pos: int32 [16384], P(('grp', 'seq')), parts along dimension 0, may hold values from 0 to 4095, as said below
- tile_count: int32 [32], P(('grp', 'seq')), parts along dimension 0, may hold values from 0 to 512, as said below
- slide_weight: bfloat16 [1536, 1536], replicated, may hold values from -0.15625 to 0.15625
- slide_bias: float32 [1536], replicated, may hold values from -3 to 3
- norm_gain: float32 [1536], replicated, may hold values from 0.5 to 1.5
- in_weight: bfloat16 [1536, 3328], replicated, may hold values from -0.15625 to 0.15625
- dt_weight: bfloat16 [1536, 24], replicated, may hold values from -0.15625 to 0.15625
- conv_weight: float32 [2, 4, 1792], replicated, may hold values from -0.6 to 0.6
- conv_bias: float32 [2, 1792], replicated, may hold values from -0.5 to 0.1
- dt_bias: float32 [2, 24], replicated, may hold values from -10.5 to -4
- a_log: float32 [2, 24], replicated, may hold values from 0 to 1.5
- out_gain: float32 [1536], replicated, may hold values from 0.5 to 1.5
- out_weight: bfloat16 [1536, 1536], replicated, may hold values from -0.15625 to 0.15625
Outputs:
- hidden: bfloat16 [8192, 1536], P(('grp', 'seq')), parts along dimension 0
The draws below stay inside these ranges and needn't reach their ends.
There are 2 independent parts, one for each index of `grp`. The reference program is written for one: setup_inputs(seed, part) draws one part's arguments, and reference() takes and returns one part's arrays. A program takes and returns all parts, laid end to end along the dimension named above; an argument that names none is the same for every part. Nothing has to cross between parts.
Inputs may be any that keep to these rules, and one draw needn't show every extreme that they name: The live slots of all readers together hold every slide position exactly once; the position's owner is tile_pos // 256. A reader with live slots holds the same number for every owner, at most 32, and 32 is reached in every draw. Slots beyond a reader's count hold arbitrary positions. `tile_count`: A quarter of the readers hold 512 live tiles, half of them 256, the rest none; which readers is drawn.
All inputs are finite; a program needn't handle non-finite values.
Results may differ from the reference program's by a relative error of at most 0.009.
Values may be sent and summed in bfloat16 or wider, within the bound.
No kernel may reach another device: no remote copies, remote signals or barrier semaphores. Data moves between devices by JAX's collectives and lax.ppermute only.
A program may use at most 192 MiB of HBM per device.

```python
import jax
import jax.numpy as jnp
from jax import lax

D = 1536
E = 1536
HEAD_DIM = 64
NS = 128
KERNEL = 4
BLOCK = 128
SEQ_DEV = 256
HEADS = 24
TOTAL = 4096
SLOTS = 512
CAP = 32


cluster_count = 64


def layout(key):
    readers = TOTAL // SEQ_DEV
    share = SEQ_DEV // readers
    ranks = jnp.arange(readers, dtype=jnp.int32)
    levels = jnp.where(ranks < readers // 4, 2 * share, jnp.where(ranks < 3 * readers // 4, share, 0)).astype(jnp.int32)
    starts = jnp.cumsum(levels) - levels
    order = jax.random.permutation(jax.random.fold_in(key, 11), readers)
    placed = jnp.argsort(order)
    counts = levels[placed]
    begins = starts[placed]
    owner_keys = jax.random.split(jax.random.fold_in(key, 12), readers)
    shuffles = jax.vmap(lambda k: jax.random.permutation(k, SEQ_DEV))(owner_keys)
    positions = jnp.arange(CAP, dtype=jnp.int32)
    picks = jnp.minimum(begins[:, None] + positions[None, :], SEQ_DEV - 1)
    chosen = shuffles[:, picks]
    owners = jnp.arange(readers, dtype=jnp.int32)
    spots = owners[:, None, None] * SEQ_DEV + chosen
    spots = jnp.transpose(spots, (1, 0, 2)).reshape(readers, SLOTS)
    usable = jnp.broadcast_to(positions[None, None, :] < counts[:, None, None], (readers, readers, CAP)).reshape(readers, SLOTS)
    mix_keys = jax.random.split(jax.random.fold_in(key, 13), readers)
    noise = jax.vmap(lambda k: jax.random.permutation(k, SLOTS))(mix_keys)
    sort_keys = jnp.where(usable, 0, SLOTS) + noise
    arrange = jnp.argsort(sort_keys, axis=1)
    spots = jnp.take_along_axis(spots, arrange, axis=1)
    filler = jax.random.randint(jax.random.fold_in(key, 14), (readers, SLOTS), 0, TOTAL)
    slot_ids = jnp.arange(SLOTS, dtype=jnp.int32)
    live_counts = readers * counts
    spots = jnp.where(slot_ids[None, :] < live_counts[:, None], spots, filler)
    return (spots.reshape(-1).astype(jnp.int32), live_counts.astype(jnp.int32))


def draw_tile_pos(key, part):
    return layout(key)[0]


def draw_tile_count(key, part):
    return layout(key)[1]


def draw_tile_embeds(key, part):
    readers = TOTAL // SEQ_DEV
    rows = readers * SLOTS
    labels = jax.random.randint(jax.random.fold_in(key, 21), (rows,), 0, cluster_count)
    centers = 0.85 * jax.random.normal(jax.random.fold_in(key, 22), (cluster_count, D), jnp.float32)
    spread = 0.5 * jax.random.normal(jax.random.fold_in(key, 23), (rows, D), jnp.float32)
    values = centers[labels] + spread
    return jnp.clip(values, -6.0, 6.0).astype(jnp.bfloat16)


def centred(stream_key, extent, width, most, held_as=jnp.bfloat16):
    values = jax.random.normal(stream_key, extent, jnp.float32) * width
    return jnp.minimum(jnp.maximum(values, -most), most).astype(held_as)


def setup_inputs(seed: int = 0, part: int = 0) -> dict:
    seeds = jax.random.split(jax.random.key(seed), 15)
    part_splits = jax.random.split(jax.random.fold_in(seeds[14], part), 15)
    return {
        "tile_embeds": draw_tile_embeds(jax.random.fold_in(jax.random.fold_in(seeds[14], part), 71), part),
        "tile_pos": draw_tile_pos(jax.random.fold_in(jax.random.fold_in(seeds[14], part), 71), part),
        "tile_count": draw_tile_count(jax.random.fold_in(jax.random.fold_in(seeds[14], part), 71), part),
        "slide_weight": centred(seeds[3], (D, D), D ** -0.5, 0.15625),
        "slide_bias": centred(seeds[4], (D,), 0.5, 3.0, jnp.float32),
        "norm_gain": jnp.clip(1.0 + 0.1 * jax.random.normal(seeds[5], (D,), jnp.float32), 0.5, 1.5),
        "in_weight": centred(seeds[6], (D, 2 * E + 2 * NS), D ** -0.5, 0.15625),
        "dt_weight": centred(seeds[7], (D, HEADS), D ** -0.5, 0.15625),
        "conv_weight": jnp.clip(jax.random.uniform(seeds[8], (2, KERNEL, E + 2 * NS), jnp.float32, -0.6, 0.6), -0.6, 0.6),
        "conv_bias": jnp.clip(jax.random.uniform(seeds[9], (2, E + 2 * NS), jnp.float32, -0.5, 0.1), -0.5, 0.1),
        "dt_bias": jnp.clip(jax.random.uniform(seeds[10], (2, HEADS), jnp.float32, -10.5, -4.0), -10.5, -4.0),
        "a_log": jnp.clip(jax.random.uniform(seeds[11], (2, HEADS), jnp.float32, 0.0, 1.5), 0.0, 1.5),
        "out_gain": jnp.clip(1.0 + 0.1 * jax.random.normal(seeds[12], (E,), jnp.float32), 0.5, 1.5),
        "out_weight": centred(seeds[13], (E, D), E ** -0.5, 0.15625),
    }


precise = lax.Precision.HIGHEST
epsilon = 1e-05

def rms_scale(values, scale_gain):
    mean_sq = lax.optimization_barrier(jnp.mean(values * values, axis=-1, keepdims=True))
    return values * lax.rsqrt(mean_sq + epsilon) * scale_gain

def sweep(signal, write_map, read_map, step_size, decay_rate):
    blocks = signal.shape[0] // BLOCK
    signal = signal.reshape(blocks, BLOCK, HEADS, HEAD_DIM)
    write_map = write_map.reshape(blocks, BLOCK, NS)
    read_map = read_map.reshape(blocks, BLOCK, NS)
    step_size = step_size.reshape(blocks, BLOCK, HEADS)
    positions = jnp.arange(BLOCK)
    causal_mask = positions[:, None] >= positions[None, :]

    def advance(state, item):
        signal_b, write_b, read_b, size_b = item
        log_decay = jnp.cumsum(size_b * decay_rate, axis=0)
        decay_turned = log_decay.T
        log_gaps = decay_turned[:, :, None] - decay_turned[:, None, :]
        weights = jnp.exp(jnp.where(causal_mask[None], log_gaps, -1e+30))
        scores = jnp.dot(read_b, write_b.T, precision=precise)
        mixing = scores[None] * weights * size_b.T[:, None, :]
        within = jnp.einsum('hts,shp->thp', mixing, signal_b, precision=precise)
        carried = jnp.einsum('tn,hpn->thp', read_b, state, precision=precise) * jnp.exp(log_decay)[:, :, None]
        tail_weight = jnp.exp(log_decay[-1][None, :] - log_decay) * size_b
        fresh_state = jnp.einsum('sh,shp,sn->hpn', tail_weight, signal_b, write_b, precision=precise)
        new_state = jnp.exp(log_decay[-1])[:, None, None] * state + fresh_state
        return (new_state, within + carried)
    start = jnp.zeros((HEADS, HEAD_DIM, NS), jnp.float32)
    final_state, result = lax.scan(advance, start, (signal, write_map, read_map, step_size))
    return result.reshape(-1, HEADS * HEAD_DIM)

def reference(tile_embeds, tile_pos, tile_count, slide_weight, slide_bias, norm_gain, in_weight, dt_weight, conv_weight, conv_bias, dt_bias, a_log, out_gain, out_weight):
    slot_index = jnp.arange(tile_embeds.shape[0]).astype(jnp.int32)
    reader = (slot_index // SLOTS).astype(jnp.int32)
    is_live = slot_index % SLOTS < tile_count[reader]
    target = jnp.where(is_live, tile_pos, TOTAL).astype(jnp.int32)
    tiles = jnp.zeros((TOTAL + 1, D), jnp.bfloat16).at[target].set(tile_embeds)[:TOTAL]
    embedded = (jnp.dot(tiles, slide_weight, preferred_element_type=jnp.float32) + slide_bias).astype(jnp.bfloat16)
    normed = rms_scale(embedded.astype(jnp.float32), norm_gain).astype(jnp.bfloat16)
    projected = jnp.dot(normed, in_weight, preferred_element_type=jnp.float32).astype(jnp.bfloat16)
    dt_raw = jnp.dot(normed, dt_weight, preferred_element_type=jnp.float32)
    gate_part = projected[:, :E].astype(jnp.float32)
    conv_input = projected[:, E:]
    padded = jnp.pad(conv_input, ((KERNEL - 1, KERNEL - 1), (0, 0))).astype(jnp.float32)
    total = jnp.zeros((TOTAL, E), jnp.float32)
    for direction in range(2):
        summed = conv_bias[direction] + jnp.zeros((TOTAL, E + 2 * NS), jnp.float32)
        for offset in range(KERNEL):
            first = offset if direction == 0 else 2 * (KERNEL - 1) - offset
            summed = summed + conv_weight[direction, offset] * padded[first:first + TOTAL]
        activated = jax.nn.silu(summed)
        step_size = jax.nn.softplus(dt_raw + dt_bias[direction])
        decay_rate = -jnp.exp(a_log[direction])
        if direction == 1:
            activated = jnp.flip(activated, 0)
            step_size = jnp.flip(step_size, 0)
        result = sweep(activated[:, :E], activated[:, E:E + NS], activated[:, E + NS:], step_size, decay_rate)
        if direction == 1:
            result = jnp.flip(result, 0)
        total = total + result
    gated = total * jax.nn.silu(gate_part)
    mixed = rms_scale(gated, out_gain).astype(jnp.bfloat16)
    hidden = embedded.astype(jnp.float32) + jnp.dot(mixed, out_weight, preferred_element_type=jnp.float32)
    return hidden.astype(jnp.bfloat16)
```

```python
import jax
import jax.numpy as jnp
from jax import lax
from jax.sharding import PartitionSpec as P

E = 1536
HEAD_DIM = 64
NS = 128
KERNEL = 4
HEADS = 24


precise = lax.Precision.HIGHEST
epsilon = 1e-05


def rms_scale(values, scale_gain):
    mean_sq = jnp.mean(values * values, axis=-1, keepdims=True)
    return values * lax.rsqrt(mean_sq + epsilon) * scale_gain


def route_tiles(tile_embeds, tile_pos, tile_count, devices, rows):
    slots, width = tile_embeds.shape
    capacity = slots // devices
    is_live = jnp.arange(slots, dtype=jnp.int32) < tile_count[0]
    owners = jnp.where(is_live, tile_pos // rows, devices)
    one_hot = (owners[:, None] == jnp.arange(devices, dtype=jnp.int32)[None, :]).astype(jnp.int32)
    ranking = jnp.sum(jnp.cumsum(one_hot, axis=0) * one_hot, axis=1) - 1
    target = jnp.where(is_live, owners * capacity + ranking, -1)
    match = target[None, :] == jnp.arange(devices * capacity, dtype=jnp.int32)[:, None]
    send = jnp.dot(match.astype(jnp.bfloat16), tile_embeds, preferred_element_type=jnp.float32)
    send = send.astype(jnp.bfloat16).reshape(devices, capacity, width)
    send_rows = jnp.sum(jnp.where(match, (tile_pos % rows + 1)[None, :], 0), axis=1) - 1
    arrived = lax.all_to_all(send, "seq", 0, 0, tiled=True).reshape(devices * capacity, width)
    arrived_rows = lax.all_to_all(
        send_rows.reshape(devices, capacity), "seq", 0, 0, tiled=True
    ).reshape(devices * capacity)
    place = arrived_rows[None, :] == jnp.arange(rows, dtype=jnp.int32)[:, None]
    tiles = jnp.dot(place.astype(jnp.bfloat16), arrived, preferred_element_type=jnp.float32)
    return tiles.astype(jnp.bfloat16)


def halo(shard, width):
    size = lax.axis_size("seq")
    up = [(i, i + 1) for i in range(size - 1)]
    down = [(i + 1, i) for i in range(size - 1)]
    before = lax.ppermute(shard[-width:], "seq", up)
    after = lax.ppermute(shard[:width], "seq", down)
    return jnp.concatenate([before, shard, after], axis=0)


def local_terms(activated, step_size, decay_rate, backward):
    rows = activated.shape[0]
    signal = activated[:, :E].reshape(rows, HEADS, HEAD_DIM)
    write_map = activated[:, E : E + NS]
    read_map = activated[:, E + NS :]
    log_step = step_size * decay_rate
    log_decay = lax.cumsum(log_step, axis=0, reverse=backward)
    positions = jnp.arange(rows)
    if backward:
        mask = positions[:, None] <= positions[None, :]
        edge = log_decay[0]
    else:
        mask = positions[:, None] >= positions[None, :]
        edge = log_decay[-1]
    turned = log_decay.T
    gaps = turned[:, :, None] - turned[:, None, :]
    weights = jnp.exp(jnp.where(mask[None], gaps, -1e30))
    scores = jnp.dot(read_map, write_map.T, precision=precise)
    mixing = scores[None] * weights * step_size.T[:, None, :]
    within = jnp.einsum("hts,shp->thp", mixing, signal, precision=precise)
    tail_weight = jnp.exp(edge[None, :] - log_decay) * step_size
    own_state = jnp.einsum(
        "shp,sn->hpn", tail_weight[:, :, None] * signal, write_map, precision=precise
    )
    return within, own_state, jnp.exp(edge), jnp.exp(log_decay), read_map


def exchange(decay, state, backward):
    size, me = lax.axis_size("seq"), lax.axis_index("seq")
    done_decay = jnp.ones_like(decay)
    done_state = jnp.zeros_like(state)
    run_decay, run_state = decay, state
    shift = 1
    while shift < size:
        if backward:
            pairs = [(i + shift, i) for i in range(size - shift)]
            valid = me + shift < size
        else:
            pairs = [(i, i + shift) for i in range(size - shift)]
            valid = me >= shift
        got_state = lax.ppermute(run_state.astype(jnp.bfloat16), "seq", pairs).astype(jnp.float32)
        got_decay = jnp.where(valid, lax.ppermute(run_decay, "seq", pairs), 1.0)
        done_state = done_decay[:, None, None] * got_state + done_state
        done_decay = got_decay * done_decay
        if 2 * shift < size:
            run_state = run_decay[:, None, None] * got_state + run_state
            run_decay = got_decay * run_decay
        shift *= 2
    return done_state


def per_device(
    tile_embeds,
    tile_pos,
    tile_count,
    slide_weight,
    slide_bias,
    norm_gain,
    in_weight,
    dt_weight,
    conv_weight,
    conv_bias,
    dt_bias,
    a_log,
    out_gain,
    out_weight,
):
    devices = lax.axis_size("seq")
    rows = tile_embeds.shape[0] // 2
    tiles = route_tiles(tile_embeds, tile_pos, tile_count, devices, rows)
    embedded = (
        jnp.dot(tiles, slide_weight, preferred_element_type=jnp.float32) + slide_bias
    ).astype(jnp.bfloat16)
    normed = rms_scale(embedded.astype(jnp.float32), norm_gain).astype(jnp.bfloat16)
    projected = jnp.dot(normed, in_weight, preferred_element_type=jnp.float32).astype(jnp.bfloat16)
    dt_raw = jnp.dot(normed, dt_weight, preferred_element_type=jnp.float32)
    gate_part = projected[:, :E].astype(jnp.float32)
    conv_input = projected[:, E:]
    padded = halo(conv_input, KERNEL - 1).astype(jnp.float32)
    parts = []
    for direction in range(2):
        summed = conv_bias[direction] + jnp.zeros((rows, conv_input.shape[1]), jnp.float32)
        for offset in range(KERNEL):
            first = offset if direction == 0 else 2 * (KERNEL - 1) - offset
            summed = summed + conv_weight[direction, offset] * padded[first : first + rows]
        activated = jax.nn.silu(summed)
        step_size = jax.nn.softplus(dt_raw + dt_bias[direction])
        decay_rate = -jnp.exp(a_log[direction])
        parts.append(local_terms(activated, step_size, decay_rate, direction == 1))
    total = jnp.zeros((rows, E), jnp.float32)
    for direction in range(2):
        within, own_state, device_decay, decay_to, read_map = parts[direction]
        incoming = exchange(device_decay, own_state, direction == 1)
        carried = (
            jnp.einsum("tn,hpn->thp", read_map, incoming, precision=precise)
            * decay_to[:, :, None]
        )
        total = total + (within + carried).reshape(rows, E)
    gated = total * jax.nn.silu(gate_part)
    mixed = rms_scale(gated, out_gain).astype(jnp.bfloat16)
    hidden = embedded.astype(jnp.float32) + jnp.dot(
        mixed, out_weight, preferred_element_type=jnp.float32
    )
    return hidden.astype(jnp.bfloat16)


def solution(mesh):
    return jax.shard_map(
        per_device,
        mesh=mesh,
        in_specs=(
            P(("grp", "seq"), None),
            P(("grp", "seq")),
            P(("grp", "seq")),
            P(),
            P(),
            P(),
            P(),
            P(),
            P(),
            P(),
            P(),
            P(),
            P(),
            P(),
        ),
        out_specs=P(("grp", "seq"), None),
        check_vma=False,
    )
```

```python
import jax
import jax.numpy as jnp
from jax import lax
from jax.sharding import PartitionSpec as P

E = 1536
HEAD_DIM = 64
NS = 128
KERNEL = 4
HEADS = 24


precise = lax.Precision.HIGHEST
epsilon = 1e-05


def rms_scale(values, scale_gain):
    mean_sq = jnp.mean(values * values, axis=-1, keepdims=True)
    return values * lax.rsqrt(mean_sq + epsilon) * scale_gain


def route_tiles(tile_embeds, tile_pos, tile_count, devices, rows):
    slots, width = tile_embeds.shape
    capacity = slots // devices
    is_live = jnp.arange(slots, dtype=jnp.int32) < tile_count[0]
    owners = jnp.where(is_live, tile_pos // rows, devices)
    one_hot = (owners[:, None] == jnp.arange(devices, dtype=jnp.int32)[None, :]).astype(jnp.int32)
    ranking = jnp.sum(jnp.cumsum(one_hot, axis=0) * one_hot, axis=1) - 1
    target = jnp.where(is_live, owners * capacity + ranking, -1)
    match = target[None, :] == jnp.arange(devices * capacity, dtype=jnp.int32)[:, None]
    row_column = (tile_pos % rows + 1).astype(jnp.bfloat16)[:, None]
    source = jnp.concatenate(
        [tile_embeds, jnp.pad(row_column, ((0, 0), (0, 127)))], axis=1
    )
    send = jnp.dot(match.astype(jnp.bfloat16), source, preferred_element_type=jnp.float32)
    send = send.astype(jnp.bfloat16).reshape(devices, capacity, width + 128)
    arrived = lax.all_to_all(send, "seq", 0, 0, tiled=True).reshape(devices * capacity, width + 128)
    arrived_rows = arrived[:, width].astype(jnp.float32).astype(jnp.int32) - 1
    place = arrived_rows[None, :] == jnp.arange(rows, dtype=jnp.int32)[:, None]
    tiles = jnp.dot(
        place.astype(jnp.bfloat16), arrived[:, :width], preferred_element_type=jnp.float32
    )
    return tiles.astype(jnp.bfloat16)


def halo(shard, width):
    size = lax.axis_size("seq")
    up = [(i, i + 1) for i in range(size - 1)]
    down = [(i + 1, i) for i in range(size - 1)]
    before = lax.ppermute(shard[-width:], "seq", up)
    after = lax.ppermute(shard[:width], "seq", down)
    return jnp.concatenate([before, shard, after], axis=0)


def local_terms(activated, step_size, decay_rate, backward):
    rows = activated.shape[0]
    signal = activated[:, :E].reshape(rows, HEADS, HEAD_DIM)
    write_map = activated[:, E : E + NS]
    read_map = activated[:, E + NS :]
    log_step = step_size * decay_rate
    log_decay = lax.cumsum(log_step, axis=0, reverse=backward)
    positions = jnp.arange(rows)
    if backward:
        mask = positions[:, None] <= positions[None, :]
        edge = log_decay[0]
    else:
        mask = positions[:, None] >= positions[None, :]
        edge = log_decay[-1]
    turned = log_decay.T
    gaps = turned[:, :, None] - turned[:, None, :]
    weights = jnp.exp(jnp.where(mask[None], gaps, -1e30))
    scores = jnp.dot(read_map, write_map.T, precision=precise)
    mixing = scores[None] * weights * step_size.T[:, None, :]
    within = jnp.einsum("hts,shp->thp", mixing, signal, precision=precise)
    tail_weight = jnp.exp(edge[None, :] - log_decay) * step_size
    own_state = jnp.einsum(
        "shp,sn->hpn", tail_weight[:, :, None] * signal, write_map, precision=precise
    )
    return within, own_state, jnp.exp(edge), jnp.exp(log_decay), read_map


def combine(earlier, later):
    return (earlier[0] * later[0], later[0][:, None, None] * earlier[1] + later[1])


def transfer(pair, pairs):
    decay, state = pair
    high = decay.astype(jnp.bfloat16)
    low = (decay - high.astype(jnp.float32)).astype(jnp.bfloat16)
    extra = jnp.stack([high, low])
    extra = jnp.pad(extra, ((0, state.shape[1] - 2), (0, state.shape[2] - decay.shape[0])))
    payload = jnp.concatenate([state.astype(jnp.bfloat16), extra[None]], axis=0)
    got = lax.ppermute(payload, "seq", pairs)
    heads = decay.shape[0]
    got_decay = got[heads, 0, :heads].astype(jnp.float32) + got[heads, 1, :heads].astype(jnp.float32)
    return got_decay, got[:heads].astype(jnp.float32)


def exchange(forward, backward):
    size, me = lax.axis_size("seq"), lax.axis_index("seq")
    chips, chip, is_one = size // 2, me // 2, me % 2 == 1
    swap = [(2 * k + d, 2 * k + 1 - d) for k in range(chips) for d in range(2)]
    pick = lambda a, b: jax.tree.map(lambda x, y: jnp.where(is_one, x, y), a, b)
    mine = pick(forward, backward)
    first = transfer(pick(backward, forward), swap)
    run = combine(first, mine)
    done = (jnp.ones_like(mine[0]), jnp.zeros_like(mine[1]))
    shift = 1
    while shift < chips:
        pairs = [(2 * k + 1, 2 * (k + shift) + 1) for k in range(chips - shift)]
        pairs += [(2 * (k + shift), 2 * k) for k in range(chips - shift)]
        valid = jnp.where(is_one, chip >= shift, chip + shift < chips)
        got_decay, got_state = transfer(run, pairs)
        got = (jnp.where(valid, got_decay, 1.0), got_state)
        done = combine(got, done)
        if 2 * shift < chips:
            run = combine(got, run)
        shift *= 2
    other = lax.ppermute(done[1].astype(jnp.bfloat16), "seq", swap).astype(jnp.float32)
    mine_in = first[0][:, None, None] * done[1] + first[1]
    return jnp.where(is_one, mine_in, other), jnp.where(is_one, other, mine_in)


def per_device(
    tile_embeds,
    tile_pos,
    tile_count,
    slide_weight,
    slide_bias,
    norm_gain,
    in_weight,
    dt_weight,
    conv_weight,
    conv_bias,
    dt_bias,
    a_log,
    out_gain,
    out_weight,
):
    devices = lax.axis_size("seq")
    rows = tile_embeds.shape[0] // 2
    tiles = route_tiles(tile_embeds, tile_pos, tile_count, devices, rows)
    embedded = (
        jnp.dot(tiles, slide_weight, preferred_element_type=jnp.float32) + slide_bias
    ).astype(jnp.bfloat16)
    normed = rms_scale(embedded.astype(jnp.float32), norm_gain).astype(jnp.bfloat16)
    projected = jnp.dot(normed, in_weight, preferred_element_type=jnp.float32).astype(jnp.bfloat16)
    dt_raw = jnp.dot(normed, dt_weight, preferred_element_type=jnp.float32)
    gate_part = projected[:, :E].astype(jnp.float32)
    conv_input = projected[:, E:]
    padded = halo(conv_input, KERNEL - 1).astype(jnp.float32)
    parts = []
    for direction in range(2):
        summed = conv_bias[direction] + jnp.zeros((rows, conv_input.shape[1]), jnp.float32)
        for offset in range(KERNEL):
            first = offset if direction == 0 else 2 * (KERNEL - 1) - offset
            summed = summed + conv_weight[direction, offset] * padded[first : first + rows]
        activated = jax.nn.silu(summed)
        step_size = jax.nn.softplus(dt_raw + dt_bias[direction])
        decay_rate = -jnp.exp(a_log[direction])
        parts.append(local_terms(activated, step_size, decay_rate, direction == 1))
    incomings = exchange(
        (parts[0][2], parts[0][1]), (parts[1][2], parts[1][1])
    )
    total = jnp.zeros((rows, E), jnp.float32)
    for direction in range(2):
        within, own_state, device_decay, decay_to, read_map = parts[direction]
        incoming = incomings[direction]
        carried = (
            jnp.einsum("tn,hpn->thp", read_map, incoming, precision=precise)
            * decay_to[:, :, None]
        )
        total = total + (within + carried).reshape(rows, E)
    gated = total * jax.nn.silu(gate_part)
    mixed = rms_scale(gated, out_gain).astype(jnp.bfloat16)
    hidden = embedded.astype(jnp.float32) + jnp.dot(
        mixed, out_weight, preferred_element_type=jnp.float32
    )
    return hidden.astype(jnp.bfloat16)


def solution(mesh):
    return jax.shard_map(
        per_device,
        mesh=mesh,
        in_specs=(
            P(("grp", "seq"), None),
            P(("grp", "seq")),
            P(("grp", "seq")),
            P(),
            P(),
            P(),
            P(),
            P(),
            P(),
            P(),
            P(),
            P(),
            P(),
            P(),
        ),
        out_specs=P(("grp", "seq"), None),
        check_vma=False,
    )
```

```python
import jax
import jax.numpy as jnp
from jax import lax
from jax.sharding import PartitionSpec as P

E = 1536
HEAD_DIM = 64
NS = 128
KERNEL = 4
HEADS = 24


fast = lax.Precision.HIGH
epsilon = 1e-05


def rms_scale(values, scale_gain):
    mean_sq = jnp.mean(values * values, axis=-1, keepdims=True)
    return values * lax.rsqrt(mean_sq + epsilon) * scale_gain


def route_tiles(tile_embeds, tile_pos, tile_count, devices, rows):
    slots, width = tile_embeds.shape
    capacity = slots // devices
    is_live = jnp.arange(slots, dtype=jnp.int32) < tile_count[0]
    owners = jnp.where(is_live, tile_pos // rows, devices)
    one_hot = (owners[:, None] == jnp.arange(devices, dtype=jnp.int32)[None, :]).astype(jnp.int32)
    ranking = jnp.sum(jnp.cumsum(one_hot, axis=0) * one_hot, axis=1) - 1
    target = jnp.where(is_live, owners * capacity + ranking, -1)
    match = target[None, :] == jnp.arange(devices * capacity, dtype=jnp.int32)[:, None]
    row_column = (tile_pos % rows + 1).astype(jnp.bfloat16)[:, None]
    source = jnp.concatenate(
        [tile_embeds, jnp.pad(row_column, ((0, 0), (0, 127)))], axis=1
    )
    send = jnp.dot(match.astype(jnp.bfloat16), source, preferred_element_type=jnp.float32)
    send = send.astype(jnp.bfloat16).reshape(devices, capacity, width + 128)
    arrived = lax.all_to_all(send, "seq", 0, 0, tiled=True).reshape(devices * capacity, width + 128)
    arrived_rows = arrived[:, width].astype(jnp.float32).astype(jnp.int32) - 1
    place = arrived_rows[None, :] == jnp.arange(rows, dtype=jnp.int32)[:, None]
    tiles = jnp.dot(
        place.astype(jnp.bfloat16), arrived[:, :width], preferred_element_type=jnp.float32
    )
    return tiles.astype(jnp.bfloat16)


def halo(shard, width):
    size = lax.axis_size("seq")
    up = [(i, i + 1) for i in range(size - 1)]
    down = [(i + 1, i) for i in range(size - 1)]
    before = lax.ppermute(shard[:, -width:].T, "seq", up).T
    after = lax.ppermute(shard[:, :width].T, "seq", down).T
    return jnp.concatenate([before, shard, after], axis=1)


def local_terms(activated, step_size, decay_rate, backward):
    rows = activated.shape[1]
    signal = activated[:E].reshape(HEADS, HEAD_DIM, rows)
    write_map = activated[E : E + NS]
    read_map = activated[E + NS :]
    log_step = step_size * decay_rate[:, None]
    log_decay = lax.cumsum(log_step, axis=1, reverse=backward)
    positions = jnp.arange(rows)
    if backward:
        mask = positions[:, None] <= positions[None, :]
        edge = log_decay[:, :1]
    else:
        mask = positions[:, None] >= positions[None, :]
        edge = log_decay[:, -1:]
    gaps = log_decay[:, :, None] - log_decay[:, None, :]
    weights = jnp.exp(jnp.where(mask[None], gaps, -1e30))
    scores = lax.dot_general(read_map, write_map, (((0,), (0,)), ((), ())), precision=fast)
    mixing = scores[None] * weights * step_size[:, None, :]
    within = lax.dot_general(signal, mixing, (((2,), (2,)), ((0,), (0,))), precision=fast)
    tail_weight = jnp.exp(edge - log_decay) * step_size
    own_state = lax.dot_general(
        signal * tail_weight[:, None, :], write_map, (((2,), (1,)), ((), ())), precision=fast
    )
    return within, own_state, jnp.exp(edge[:, 0]), jnp.exp(log_decay), read_map


def combine(earlier, later):
    return (earlier[0] * later[0], later[0][:, None, None] * earlier[1] + later[1])


def transfer(pair, pairs):
    decay, state = pair
    high = decay.astype(jnp.bfloat16)
    low = (decay - high.astype(jnp.float32)).astype(jnp.bfloat16)
    extra = jnp.stack([high, low])
    extra = jnp.pad(extra, ((0, state.shape[1] - 2), (0, state.shape[2] - decay.shape[0])))
    payload = jnp.concatenate([state.astype(jnp.bfloat16), extra[None]], axis=0)
    got = lax.ppermute(payload, "seq", pairs)
    heads = decay.shape[0]
    got_decay = got[heads, 0, :heads].astype(jnp.float32) + got[heads, 1, :heads].astype(jnp.float32)
    return got_decay, got[:heads].astype(jnp.float32)


def exchange(forward, backward):
    size, me = lax.axis_size("seq"), lax.axis_index("seq")
    chips, chip, is_one = size // 2, me // 2, me % 2 == 1
    swap = [(2 * k + d, 2 * k + 1 - d) for k in range(chips) for d in range(2)]
    pick = lambda a, b: jax.tree.map(lambda x, y: jnp.where(is_one, x, y), a, b)
    mine = pick(forward, backward)
    first = transfer(pick(backward, forward), swap)
    run = combine(first, mine)
    done = (jnp.ones_like(mine[0]), jnp.zeros_like(mine[1]))
    shift = 1
    while shift < chips:
        pairs = [(2 * k + 1, 2 * (k + shift) + 1) for k in range(chips - shift)]
        pairs += [(2 * (k + shift), 2 * k) for k in range(chips - shift)]
        valid = jnp.where(is_one, chip >= shift, chip + shift < chips)
        got_decay, got_state = transfer(run, pairs)
        got = (jnp.where(valid, got_decay, 1.0), got_state)
        done = combine(got, done)
        if 2 * shift < chips:
            run = combine(got, run)
        shift *= 2
    other = lax.ppermute(done[1].astype(jnp.bfloat16), "seq", swap).astype(jnp.float32)
    mine_in = first[0][:, None, None] * done[1] + first[1]
    return jnp.where(is_one, mine_in, other), jnp.where(is_one, other, mine_in)


def per_device(
    tile_embeds,
    tile_pos,
    tile_count,
    slide_weight,
    slide_bias,
    norm_gain,
    in_weight,
    dt_weight,
    conv_weight,
    conv_bias,
    dt_bias,
    a_log,
    out_gain,
    out_weight,
):
    devices = lax.axis_size("seq")
    rows = tile_embeds.shape[0] // 2
    tiles = route_tiles(tile_embeds, tile_pos, tile_count, devices, rows)
    embedded = (
        jnp.dot(tiles, slide_weight, preferred_element_type=jnp.float32) + slide_bias
    ).astype(jnp.bfloat16)
    normed = rms_scale(embedded.astype(jnp.float32), norm_gain).astype(jnp.bfloat16)
    turned = (((0,), (1,)), ((), ()))
    projected = lax.dot_general(
        in_weight, normed, turned, preferred_element_type=jnp.float32
    ).astype(jnp.bfloat16)
    dt_raw = lax.dot_general(dt_weight, normed, turned, preferred_element_type=jnp.float32)
    gate_part = projected[:E].astype(jnp.float32)
    conv_input = projected[E:]
    padded = halo(conv_input, KERNEL - 1).astype(jnp.float32)
    parts = []
    for direction in range(2):
        summed = conv_bias[direction][:, None] + jnp.zeros((conv_input.shape[0], rows), jnp.float32)
        for offset in range(KERNEL):
            first = offset if direction == 0 else 2 * (KERNEL - 1) - offset
            summed = summed + conv_weight[direction, offset][:, None] * padded[:, first : first + rows]
        activated = jax.nn.silu(summed)
        step_size = jax.nn.softplus(dt_raw + dt_bias[direction][:, None])
        decay_rate = -jnp.exp(a_log[direction])
        parts.append(local_terms(activated, step_size, decay_rate, direction == 1))
    incomings = exchange(
        (parts[0][2], parts[0][1]), (parts[1][2], parts[1][1])
    )
    total = jnp.zeros((HEADS, HEAD_DIM, rows), jnp.float32)
    for direction in range(2):
        within, own_state, device_decay, decay_to, read_map = parts[direction]
        incoming = incomings[direction]
        carried = lax.dot_general(
            incoming, read_map, (((2,), (0,)), ((), ())), precision=fast
        ) * decay_to[:, None, :]
        total = total + within + carried
    gated = total.reshape(E, rows) * jax.nn.silu(gate_part)
    mean_sq = jnp.mean(gated * gated, axis=0, keepdims=True)
    mixed = (gated * lax.rsqrt(mean_sq + epsilon) * out_gain[:, None]).astype(jnp.bfloat16)
    hidden = embedded.astype(jnp.float32) + lax.dot_general(
        mixed, out_weight, (((0,), (0,)), ((), ())), preferred_element_type=jnp.float32
    )
    return hidden.astype(jnp.bfloat16)


def solution(mesh):
    return jax.shard_map(
        per_device,
        mesh=mesh,
        in_specs=(
            P(("grp", "seq"), None),
            P(("grp", "seq")),
            P(("grp", "seq")),
            P(),
            P(),
            P(),
            P(),
            P(),
            P(),
            P(),
            P(),
            P(),
            P(),
            P(),
        ),
        out_specs=P(("grp", "seq"), None),
        check_vma=False,
    )
```

```python
import jax
import jax.numpy as jnp
from jax import lax
from jax.sharding import PartitionSpec as P

E = 1536
HEAD_DIM = 64
NS = 128
KERNEL = 4
HEADS = 24


fast = lax.Precision.HIGH
epsilon = 1e-05


def rms_scale(values, scale_gain):
    mean_sq = jnp.mean(values * values, axis=-1, keepdims=True)
    return values * lax.rsqrt(mean_sq + epsilon) * scale_gain


def route_tiles(tile_embeds, tile_pos, tile_count, devices, rows):
    slots, width = tile_embeds.shape
    capacity = slots // devices
    is_live = jnp.arange(slots, dtype=jnp.int32) < tile_count[0]
    owners = jnp.where(is_live, tile_pos // rows, devices)
    one_hot = (owners[:, None] == jnp.arange(devices, dtype=jnp.int32)[None, :]).astype(jnp.int32)
    ranking = jnp.sum(jnp.cumsum(one_hot, axis=0) * one_hot, axis=1) - 1
    target = jnp.where(is_live, owners * capacity + ranking, -1)
    match = target[None, :] == jnp.arange(devices * capacity, dtype=jnp.int32)[:, None]
    row_column = (tile_pos % rows + 1).astype(jnp.bfloat16)[:, None]
    source = jnp.concatenate(
        [tile_embeds, jnp.pad(row_column, ((0, 0), (0, 127)))], axis=1
    )
    send = jnp.dot(match.astype(jnp.bfloat16), source, preferred_element_type=jnp.float32)
    send = send.astype(jnp.bfloat16).reshape(devices, capacity, width + 128)
    arrived = lax.all_to_all(send, "seq", 0, 0, tiled=True).reshape(devices * capacity, width + 128)
    arrived_rows = arrived[:, width].astype(jnp.float32).astype(jnp.int32) - 1
    place = arrived_rows[None, :] == jnp.arange(rows, dtype=jnp.int32)[:, None]
    tiles = jnp.dot(
        place.astype(jnp.bfloat16), arrived[:, :width], preferred_element_type=jnp.float32
    )
    return tiles.astype(jnp.bfloat16)


def halo(normed, in_weight, width):
    size = lax.axis_size("seq")
    up = [(i, i + 1) for i in range(size - 1)]
    down = [(i + 1, i) for i in range(size - 1)]
    before = lax.ppermute(normed[-width:], "seq", up)
    after = lax.ppermute(normed[:width], "seq", down)
    rows = jnp.concatenate([before, after], axis=0)
    return lax.dot_general(
        in_weight[:, E:], rows, (((0,), (1,)), ((), ())), preferred_element_type=jnp.float32
    ).astype(jnp.bfloat16)


def local_terms(activated, step_size, decay_rate, backward):
    rows = activated.shape[1]
    signal = activated[:E].reshape(HEADS, HEAD_DIM, rows)
    write_map = activated[E : E + NS]
    read_map = activated[E + NS :]
    log_step = step_size * decay_rate[:, None]
    positions = jnp.arange(rows)
    if backward:
        upper = positions[:, None] >= positions[None, :]
    else:
        upper = positions[:, None] <= positions[None, :]
    log_decay = jnp.dot(log_step, upper.astype(jnp.float32), precision=lax.Precision.HIGHEST)
    if backward:
        mask = positions[:, None] <= positions[None, :]
        edge = log_decay[:, :1]
    else:
        mask = positions[:, None] >= positions[None, :]
        edge = log_decay[:, -1:]
    gaps = log_decay[:, :, None] - log_decay[:, None, :]
    weights = jnp.exp(jnp.where(mask[None], gaps, -1e30))
    scores = lax.dot_general(read_map, write_map, (((0,), (0,)), ((), ())), precision=fast)
    mixing = scores[None] * weights * step_size[:, None, :]
    within = lax.dot_general(signal, mixing, (((2,), (2,)), ((0,), (0,))), precision=fast)
    tail_weight = jnp.exp(edge - log_decay) * step_size
    own_state = lax.dot_general(
        signal * tail_weight[:, None, :], write_map, (((2,), (1,)), ((), ())), precision=fast
    )
    return within, own_state, jnp.exp(edge[:, 0]), jnp.exp(log_decay), read_map


def combine(earlier, later):
    return (earlier[0] * later[0], later[0][:, None, None] * earlier[1] + later[1])


def transfer(pair, pairs):
    decay, state = pair
    high = decay.astype(jnp.bfloat16)
    low = (decay - high.astype(jnp.float32)).astype(jnp.bfloat16)
    extra = jnp.stack([high, low])
    extra = jnp.pad(extra, ((0, state.shape[1] - 2), (0, state.shape[2] - decay.shape[0])))
    payload = jnp.concatenate([state.astype(jnp.bfloat16), extra[None]], axis=0)
    got = lax.ppermute(payload, "seq", pairs)
    heads = decay.shape[0]
    got_decay = got[heads, 0, :heads].astype(jnp.float32) + got[heads, 1, :heads].astype(jnp.float32)
    return got_decay, got[:heads].astype(jnp.float32)


def exchange(forward, backward):
    size, me = lax.axis_size("seq"), lax.axis_index("seq")
    chips, chip, is_one = size // 2, me // 2, me % 2 == 1
    swap = [(2 * k + d, 2 * k + 1 - d) for k in range(chips) for d in range(2)]
    pick = lambda a, b: jax.tree.map(lambda x, y: jnp.where(is_one, x, y), a, b)
    mine = pick(forward, backward)
    first = transfer(pick(backward, forward), swap)
    run = combine(first, mine)
    done = (jnp.ones_like(mine[0]), jnp.zeros_like(mine[1]))
    shift = 1
    while shift < chips:
        pairs = [(2 * k + 1, 2 * (k + shift) + 1) for k in range(chips - shift)]
        pairs += [(2 * (k + shift), 2 * k) for k in range(chips - shift)]
        valid = jnp.where(is_one, chip >= shift, chip + shift < chips)
        got_decay, got_state = transfer(run, pairs)
        got = (jnp.where(valid, got_decay, 1.0), got_state)
        done = combine(got, done)
        if 2 * shift < chips:
            run = combine(got, run)
        shift *= 2
    other = lax.ppermute(done[1].astype(jnp.bfloat16), "seq", swap).astype(jnp.float32)
    mine_in = first[0][:, None, None] * done[1] + first[1]
    return jnp.where(is_one, mine_in, other), jnp.where(is_one, other, mine_in)


def per_device(
    tile_embeds,
    tile_pos,
    tile_count,
    slide_weight,
    slide_bias,
    norm_gain,
    in_weight,
    dt_weight,
    conv_weight,
    conv_bias,
    dt_bias,
    a_log,
    out_gain,
    out_weight,
):
    devices = lax.axis_size("seq")
    rows = tile_embeds.shape[0] // 2
    tiles = route_tiles(tile_embeds, tile_pos, tile_count, devices, rows)
    embedded = (
        jnp.dot(tiles, slide_weight, preferred_element_type=jnp.float32) + slide_bias
    ).astype(jnp.bfloat16)
    normed = rms_scale(embedded.astype(jnp.float32), norm_gain).astype(jnp.bfloat16)
    turned = (((0,), (1,)), ((), ()))
    projected = lax.dot_general(
        in_weight, normed, turned, preferred_element_type=jnp.float32
    ).astype(jnp.bfloat16)
    dt_raw = lax.dot_general(dt_weight, normed, turned, preferred_element_type=jnp.float32)
    gate_part = projected[:E].astype(jnp.float32)
    conv_input = projected[E:]
    sides = halo(normed, in_weight, KERNEL - 1)
    padded = jnp.concatenate(
        [sides[:, : KERNEL - 1], conv_input, sides[:, KERNEL - 1 :]], axis=1
    ).astype(jnp.float32)
    parts = []
    for direction in range(2):
        summed = conv_bias[direction][:, None] + jnp.zeros((conv_input.shape[0], rows), jnp.float32)
        for offset in range(KERNEL):
            first = offset if direction == 0 else 2 * (KERNEL - 1) - offset
            summed = summed + conv_weight[direction, offset][:, None] * padded[:, first : first + rows]
        activated = jax.nn.silu(summed)
        step_size = jax.nn.softplus(dt_raw + dt_bias[direction][:, None])
        decay_rate = -jnp.exp(a_log[direction])
        parts.append(local_terms(activated, step_size, decay_rate, direction == 1))
    incomings = exchange(
        (parts[0][2], parts[0][1]), (parts[1][2], parts[1][1])
    )
    total = jnp.zeros((HEADS, HEAD_DIM, rows), jnp.float32)
    for direction in range(2):
        within, own_state, device_decay, decay_to, read_map = parts[direction]
        incoming = incomings[direction]
        carried = lax.dot_general(
            incoming, read_map, (((2,), (0,)), ((), ())), precision=fast
        ) * decay_to[:, None, :]
        total = total + within + carried
    gated = total.reshape(E, rows) * jax.nn.silu(gate_part)
    mean_sq = jnp.mean(gated * gated, axis=0, keepdims=True)
    mixed = (gated * lax.rsqrt(mean_sq + epsilon) * out_gain[:, None]).astype(jnp.bfloat16)
    hidden = embedded.astype(jnp.float32) + lax.dot_general(
        mixed, out_weight, (((0,), (0,)), ((), ())), preferred_element_type=jnp.float32
    )
    return hidden.astype(jnp.bfloat16)


def solution(mesh):
    return jax.shard_map(
        per_device,
        mesh=mesh,
        in_specs=(
            P(("grp", "seq"), None),
            P(("grp", "seq")),
            P(("grp", "seq")),
            P(),
            P(),
            P(),
            P(),
            P(),
            P(),
            P(),
            P(),
            P(),
            P(),
            P(),
        ),
        out_specs=P(("grp", "seq"), None),
        check_vma=False,
    )
```

```python
import jax
import jax.numpy as jnp
from jax import lax
from jax.sharding import PartitionSpec as P

E = 1536
HEAD_DIM = 64
NS = 128
KERNEL = 4
HEADS = 24


fast = lax.Precision.HIGH
epsilon = 1e-05


def rms_scale(values, scale_gain):
    mean_sq = jnp.mean(values * values, axis=-1, keepdims=True)
    return values * lax.rsqrt(mean_sq + epsilon) * scale_gain


def route_tiles(tile_embeds, tile_pos, tile_count, devices, rows):
    slots, width = tile_embeds.shape
    capacity = slots // devices
    is_live = jnp.arange(slots, dtype=jnp.int32) < tile_count[0]
    owners = jnp.where(is_live, tile_pos // rows, devices)
    one_hot = (owners[:, None] == jnp.arange(devices, dtype=jnp.int32)[None, :]).astype(jnp.int32)
    ranking = jnp.sum(jnp.cumsum(one_hot, axis=0) * one_hot, axis=1) - 1
    target = jnp.where(is_live, owners * capacity + ranking, -1)
    match = target[None, :] == jnp.arange(devices * capacity, dtype=jnp.int32)[:, None]
    row_column = (tile_pos % rows + 1).astype(jnp.bfloat16)[:, None]
    source = jnp.concatenate(
        [tile_embeds, jnp.pad(row_column, ((0, 0), (0, 127)))], axis=1
    )
    send = jnp.dot(match.astype(jnp.bfloat16), source, preferred_element_type=jnp.float32)
    send = send.astype(jnp.bfloat16).reshape(devices, capacity, width + 128)
    arrived = lax.all_to_all(send, "seq", 0, 0, tiled=True).reshape(devices * capacity, width + 128)
    arrived_rows = arrived[:, width].astype(jnp.float32).astype(jnp.int32) - 1
    place = arrived_rows[None, :] == jnp.arange(rows, dtype=jnp.int32)[:, None]
    tiles = jnp.dot(
        place.astype(jnp.bfloat16), arrived[:, :width], preferred_element_type=jnp.float32
    )
    return tiles.astype(jnp.bfloat16)


def halo(normed, in_weight, width):
    size = lax.axis_size("seq")
    up = [(i, i + 1) for i in range(size - 1)]
    down = [(i + 1, i) for i in range(size - 1)]
    before = lax.ppermute(normed[-width:], "seq", up)
    after = lax.ppermute(normed[:width], "seq", down)
    rows = jnp.concatenate([before, after], axis=0)
    return lax.dot_general(
        in_weight[:, E:], rows, (((0,), (1,)), ((), ())), preferred_element_type=jnp.float32
    ).astype(jnp.bfloat16)


def local_terms(activated, step_size, decay_rate, backward):
    rows = activated.shape[1]
    signal = activated[:E].reshape(HEADS, HEAD_DIM, rows)
    write_map = activated[E : E + NS]
    read_map = activated[E + NS :]
    log_step = step_size * decay_rate[:, None]
    positions = jnp.arange(rows)
    if backward:
        upper = positions[:, None] >= positions[None, :]
    else:
        upper = positions[:, None] <= positions[None, :]
    log_decay = jnp.dot(log_step, upper.astype(jnp.float32), precision=lax.Precision.HIGHEST)
    if backward:
        mask = positions[:, None] <= positions[None, :]
        edge = log_decay[:, :1]
    else:
        mask = positions[:, None] >= positions[None, :]
        edge = log_decay[:, -1:]
    gaps = log_decay[:, :, None] - log_decay[:, None, :]
    weights = jnp.exp(jnp.where(mask[None], gaps, -1e30))
    scores = lax.dot_general(read_map, write_map, (((0,), (0,)), ((), ())), precision=fast)
    mixing = scores[None] * weights * step_size[:, None, :]
    within = lax.dot_general(signal, mixing, (((2,), (2,)), ((0,), (0,))), precision=fast)
    tail_weight = jnp.exp(edge - log_decay) * step_size
    own_state = lax.dot_general(
        signal * tail_weight[:, None, :], write_map, (((2,), (1,)), ((), ())), precision=fast
    )
    return within, own_state, jnp.exp(edge[:, 0]), jnp.exp(log_decay), read_map


def combine(earlier, later):
    return (earlier[0] * later[0], later[0][:, None, None] * earlier[1] + later[1])


def transfer(pair, pairs):
    decay, state = pair
    high = decay.astype(jnp.bfloat16)
    low = (decay - high.astype(jnp.float32)).astype(jnp.bfloat16)
    extra = jnp.stack([high, low])
    extra = jnp.pad(extra, ((0, state.shape[1] - 2), (0, state.shape[2] - decay.shape[0])))
    payload = jnp.concatenate([state.astype(jnp.bfloat16), extra[None]], axis=0)
    got = lax.ppermute(payload, "seq", pairs)
    heads = decay.shape[0]
    got_decay = got[heads, 0, :heads].astype(jnp.float32) + got[heads, 1, :heads].astype(jnp.float32)
    return got_decay, got[:heads].astype(jnp.float32)


def exchange(forward, backward, ties):
    size, me = lax.axis_size("seq"), lax.axis_index("seq")
    chips, chip, is_one = size // 2, me // 2, me % 2 == 1
    swap = [(2 * k + d, 2 * k + 1 - d) for k in range(chips) for d in range(2)]
    pick = lambda a, b: jax.tree.map(lambda x, y: jnp.where(is_one, x, y), a, b)
    mine = pick(forward, backward)
    first = transfer(pick(backward, forward), swap)
    run = combine(first, mine)
    done = (jnp.ones_like(mine[0]), jnp.zeros_like(mine[1]))
    shift, level, tied = 1, 0, []
    while shift < chips:
        if level < len(ties) and ties[level] is not None:
            run, held = lax.optimization_barrier((run, ties[level]))
            tied.append(held)
        level += 1
        pairs = [(2 * k + 1, 2 * (k + shift) + 1) for k in range(chips - shift)]
        pairs += [(2 * (k + shift), 2 * k) for k in range(chips - shift)]
        valid = jnp.where(is_one, chip >= shift, chip + shift < chips)
        got_decay, got_state = transfer(run, pairs)
        got = (jnp.where(valid, got_decay, 1.0), got_state)
        done = combine(got, done)
        if 2 * shift < chips:
            run = combine(got, run)
        shift *= 2
    other = lax.ppermute(done[1].astype(jnp.bfloat16), "seq", swap).astype(jnp.float32)
    mine_in = first[0][:, None, None] * done[1] + first[1]
    return jnp.where(is_one, mine_in, other), jnp.where(is_one, other, mine_in), tied


def per_device(
    tile_embeds,
    tile_pos,
    tile_count,
    slide_weight,
    slide_bias,
    norm_gain,
    in_weight,
    dt_weight,
    conv_weight,
    conv_bias,
    dt_bias,
    a_log,
    out_gain,
    out_weight,
):
    devices = lax.axis_size("seq")
    rows = tile_embeds.shape[0] // 2
    tiles = route_tiles(tile_embeds, tile_pos, tile_count, devices, rows)
    embedded = (
        jnp.dot(tiles, slide_weight, preferred_element_type=jnp.float32) + slide_bias
    ).astype(jnp.bfloat16)
    normed = rms_scale(embedded.astype(jnp.float32), norm_gain).astype(jnp.bfloat16)
    turned = (((0,), (1,)), ((), ()))
    conv_input = lax.dot_general(
        in_weight[:, E:], normed, turned, preferred_element_type=jnp.float32
    ).astype(jnp.bfloat16)
    dt_raw = lax.dot_general(dt_weight, normed, turned, preferred_element_type=jnp.float32)
    gate_part = lax.dot_general(
        in_weight[:, :E], normed, turned, preferred_element_type=jnp.float32
    ).astype(jnp.bfloat16).astype(jnp.float32)
    gate_silu = jax.nn.silu(gate_part)
    sides = halo(normed, in_weight, KERNEL - 1)
    padded = jnp.concatenate(
        [sides[:, : KERNEL - 1], conv_input, sides[:, KERNEL - 1 :]], axis=1
    ).astype(jnp.float32)
    parts = []
    for direction in range(2):
        summed = conv_bias[direction][:, None] + jnp.zeros((conv_input.shape[0], rows), jnp.float32)
        for offset in range(KERNEL):
            first = offset if direction == 0 else 2 * (KERNEL - 1) - offset
            summed = summed + conv_weight[direction, offset][:, None] * padded[:, first : first + rows]
        activated = jax.nn.silu(summed)
        step_size = jax.nn.softplus(dt_raw + dt_bias[direction][:, None])
        decay_rate = -jnp.exp(a_log[direction])
        parts.append(local_terms(activated, step_size, decay_rate, direction == 1))
    fwd_in, bwd_in, tied = exchange(
        (parts[0][2], parts[0][1]),
        (parts[1][2], parts[1][1]),
        [None, (gate_silu, parts[0][0]), parts[1][0]],
    )
    if len(tied) == 2:
        (gate_silu, within_fwd), within_bwd = tied
    else:
        within_fwd, within_bwd = parts[0][0], parts[1][0]
    incomings = (fwd_in, bwd_in)
    withins = (within_fwd, within_bwd)
    total = jnp.zeros((HEADS, HEAD_DIM, rows), jnp.float32)
    for direction in range(2):
        _, own_state, device_decay, decay_to, read_map = parts[direction]
        within = withins[direction]
        incoming = incomings[direction]
        carried = lax.dot_general(
            incoming, read_map, (((2,), (0,)), ((), ())), precision=fast
        ) * decay_to[:, None, :]
        total = total + within + carried
    gated = total.reshape(E, rows) * gate_silu
    mean_sq = jnp.mean(gated * gated, axis=0, keepdims=True)
    mixed = (gated * lax.rsqrt(mean_sq + epsilon) * out_gain[:, None]).astype(jnp.bfloat16)
    hidden = embedded.astype(jnp.float32) + lax.dot_general(
        mixed, out_weight, (((0,), (0,)), ((), ())), preferred_element_type=jnp.float32
    )
    return hidden.astype(jnp.bfloat16)


def solution(mesh):
    return jax.shard_map(
        per_device,
        mesh=mesh,
        in_specs=(
            P(("grp", "seq"), None),
            P(("grp", "seq")),
            P(("grp", "seq")),
            P(),
            P(),
            P(),
            P(),
            P(),
            P(),
            P(),
            P(),
            P(),
            P(),
            P(),
        ),
        out_specs=P(("grp", "seq"), None),
        check_vma=False,
    )
```

```python
import jax
import jax.numpy as jnp
from jax import lax
from jax.sharding import PartitionSpec as P

E = 1536
HEAD_DIM = 64
NS = 128
KERNEL = 4
HEADS = 24


fast = lax.Precision.HIGH
epsilon = 1e-05


def rms_scale(values, scale_gain):
    mean_sq = jnp.mean(values * values, axis=-1, keepdims=True)
    return values * lax.rsqrt(mean_sq + epsilon) * scale_gain


def route_tiles(tile_embeds, tile_pos, tile_count, devices, rows):
    slots, width = tile_embeds.shape
    capacity = slots // devices
    is_live = jnp.arange(slots, dtype=jnp.int32) < tile_count[0]
    owners = jnp.where(is_live, tile_pos // rows, devices)
    one_hot = (owners[:, None] == jnp.arange(devices, dtype=jnp.int32)[None, :]).astype(jnp.int32)
    ranking = jnp.sum(jnp.cumsum(one_hot, axis=0) * one_hot, axis=1) - 1
    target = jnp.where(is_live, owners * capacity + ranking, -1)
    match = target[None, :] == jnp.arange(devices * capacity, dtype=jnp.int32)[:, None]
    row_column = (tile_pos % rows + 1).astype(jnp.bfloat16)[:, None]
    source = jnp.concatenate(
        [tile_embeds, jnp.pad(row_column, ((0, 0), (0, 127)))], axis=1
    )
    send = jnp.dot(match.astype(jnp.bfloat16), source, preferred_element_type=jnp.float32)
    send = send.astype(jnp.bfloat16).reshape(devices, capacity, width + 128)
    arrived = lax.all_to_all(send, "seq", 0, 0, tiled=True).reshape(devices * capacity, width + 128)
    arrived_rows = arrived[:, width].astype(jnp.float32).astype(jnp.int32) - 1
    place = arrived_rows[None, :] == jnp.arange(rows, dtype=jnp.int32)[:, None]
    tiles = jnp.dot(
        place.astype(jnp.bfloat16), arrived[:, :width], preferred_element_type=jnp.float32
    )
    return tiles.astype(jnp.bfloat16)


def halo(normed, in_weight, width):
    size = lax.axis_size("seq")
    up = [(i, i + 1) for i in range(size - 1)]
    down = [(i + 1, i) for i in range(size - 1)]
    before = lax.ppermute(normed[-width:], "seq", up)
    after = lax.ppermute(normed[:width], "seq", down)
    rows = jnp.concatenate([before, after], axis=0)
    return lax.dot_general(
        in_weight[:, E:], rows, (((0,), (1,)), ((), ())), preferred_element_type=jnp.float32
    ).astype(jnp.bfloat16)


def local_terms(activated, step_size, decay_rate, backward):
    rows = activated.shape[1]
    signal = activated[:E].reshape(HEADS, HEAD_DIM, rows)
    write_map = activated[E : E + NS]
    read_map = activated[E + NS :]
    log_step = step_size * decay_rate[:, None]
    positions = jnp.arange(rows)
    if backward:
        upper = positions[:, None] >= positions[None, :]
    else:
        upper = positions[:, None] <= positions[None, :]
    log_decay = jnp.dot(log_step, upper.astype(jnp.float32), precision=lax.Precision.HIGHEST)
    if backward:
        mask = positions[:, None] <= positions[None, :]
        edge = log_decay[:, :1]
    else:
        mask = positions[:, None] >= positions[None, :]
        edge = log_decay[:, -1:]
    gaps = log_decay[:, :, None] - log_decay[:, None, :]
    weights = jnp.exp(jnp.where(mask[None], gaps, -1e30))
    scores = lax.dot_general(read_map, write_map, (((0,), (0,)), ((), ())), precision=fast)
    mixing = scores[None] * weights * step_size[:, None, :]
    within = lax.dot_general(signal, mixing, (((2,), (2,)), ((0,), (0,))), precision=fast)
    tail_weight = jnp.exp(edge - log_decay) * step_size
    own_state = lax.dot_general(
        signal * tail_weight[:, None, :], write_map, (((2,), (1,)), ((), ())), precision=fast
    )
    return within, own_state, jnp.exp(edge[:, 0]), jnp.exp(log_decay), read_map


def combine(earlier, later):
    return (earlier[0] * later[0], later[0][:, None, None] * earlier[1] + later[1])


def transfer(pair, pairs):
    decay, state = pair
    high = decay.astype(jnp.bfloat16)
    low = (decay - high.astype(jnp.float32)).astype(jnp.bfloat16)
    extra = jnp.stack([high, low])
    extra = jnp.pad(extra, ((0, state.shape[1] - 2), (0, state.shape[2] - decay.shape[0])))
    payload = jnp.concatenate([state.astype(jnp.bfloat16), extra[None]], axis=0)
    got = lax.ppermute(payload, "seq", pairs)
    heads = decay.shape[0]
    got_decay = got[heads, 0, :heads].astype(jnp.float32) + got[heads, 1, :heads].astype(jnp.float32)
    return got_decay, got[:heads].astype(jnp.float32)


def exchange(forward, backward, ties, late, late_input):
    size, me = lax.axis_size("seq"), lax.axis_index("seq")
    chips, chip, is_one = size // 2, me // 2, me % 2 == 1
    swap = [(2 * k + d, 2 * k + 1 - d) for k in range(chips) for d in range(2)]
    pick = lambda a, b: jax.tree.map(lambda x, y: jnp.where(is_one, x, y), a, b)
    mine = pick(forward, backward)
    first = transfer(pick(backward, forward), swap)
    first_state, late_input = lax.optimization_barrier((first[1], late_input))
    first = (first[0], first_state)
    ties = list(ties)
    ties[1] = (late(late_input), ties[1])
    run = combine(first, mine)
    done = (jnp.ones_like(mine[0]), jnp.zeros_like(mine[1]))
    shift, level, tied = 1, 0, []
    while shift < chips:
        if level < len(ties) and ties[level] is not None:
            run, held = lax.optimization_barrier((run, ties[level]))
            tied.append(held)
        level += 1
        pairs = [(2 * k + 1, 2 * (k + shift) + 1) for k in range(chips - shift)]
        pairs += [(2 * (k + shift), 2 * k) for k in range(chips - shift)]
        valid = jnp.where(is_one, chip >= shift, chip + shift < chips)
        got_decay, got_state = transfer(run, pairs)
        got = (jnp.where(valid, got_decay, 1.0), got_state)
        done = combine(got, done)
        if 2 * shift < chips:
            run = combine(got, run)
        shift *= 2
    other = lax.ppermute(done[1].astype(jnp.bfloat16), "seq", swap).astype(jnp.float32)
    mine_in = first[0][:, None, None] * done[1] + first[1]
    return jnp.where(is_one, mine_in, other), jnp.where(is_one, other, mine_in), tied


def per_device(
    tile_embeds,
    tile_pos,
    tile_count,
    slide_weight,
    slide_bias,
    norm_gain,
    in_weight,
    dt_weight,
    conv_weight,
    conv_bias,
    dt_bias,
    a_log,
    out_gain,
    out_weight,
):
    devices = lax.axis_size("seq")
    rows = tile_embeds.shape[0] // 2
    tiles = route_tiles(tile_embeds, tile_pos, tile_count, devices, rows)
    embedded = (
        jnp.dot(tiles, slide_weight, preferred_element_type=jnp.float32) + slide_bias
    ).astype(jnp.bfloat16)
    normed = rms_scale(embedded.astype(jnp.float32), norm_gain).astype(jnp.bfloat16)
    turned = (((0,), (1,)), ((), ()))
    conv_input = lax.dot_general(
        in_weight[:, E:], normed, turned, preferred_element_type=jnp.float32
    ).astype(jnp.bfloat16)
    dt_raw = lax.dot_general(dt_weight, normed, turned, preferred_element_type=jnp.float32)
    def gate_of(values):
        gate_part = lax.dot_general(
            in_weight[:, :E], values, turned, preferred_element_type=jnp.float32
        ).astype(jnp.bfloat16).astype(jnp.float32)
        return jax.nn.silu(gate_part)

    sides = halo(normed, in_weight, KERNEL - 1)
    padded = jnp.concatenate(
        [sides[:, : KERNEL - 1], conv_input, sides[:, KERNEL - 1 :]], axis=1
    ).astype(jnp.float32)
    parts = []
    for direction in range(2):
        summed = conv_bias[direction][:, None] + jnp.zeros((conv_input.shape[0], rows), jnp.float32)
        for offset in range(KERNEL):
            first = offset if direction == 0 else 2 * (KERNEL - 1) - offset
            summed = summed + conv_weight[direction, offset][:, None] * padded[:, first : first + rows]
        activated = jax.nn.silu(summed)
        step_size = jax.nn.softplus(dt_raw + dt_bias[direction][:, None])
        decay_rate = -jnp.exp(a_log[direction])
        parts.append(local_terms(activated, step_size, decay_rate, direction == 1))
    fwd_in, bwd_in, tied = exchange(
        (parts[0][2], parts[0][1]),
        (parts[1][2], parts[1][1]),
        [None, parts[0][0], parts[1][0]],
        gate_of,
        normed,
    )
    if len(tied) == 2:
        (gate_silu, within_fwd), within_bwd = tied
    else:
        within_fwd, within_bwd, gate_silu = parts[0][0], parts[1][0], gate_of(normed)
    incomings = (fwd_in, bwd_in)
    withins = (within_fwd, within_bwd)
    total = jnp.zeros((HEADS, HEAD_DIM, rows), jnp.float32)
    for direction in range(2):
        _, own_state, device_decay, decay_to, read_map = parts[direction]
        within = withins[direction]
        incoming = incomings[direction]
        carried = lax.dot_general(
            incoming, read_map, (((2,), (0,)), ((), ())), precision=fast
        ) * decay_to[:, None, :]
        total = total + within + carried
    gated = total.reshape(E, rows) * gate_silu
    mean_sq = jnp.mean(gated * gated, axis=0, keepdims=True)
    mixed = (gated * lax.rsqrt(mean_sq + epsilon) * out_gain[:, None]).astype(jnp.bfloat16)
    hidden = embedded.astype(jnp.float32) + lax.dot_general(
        mixed, out_weight, (((0,), (0,)), ((), ())), preferred_element_type=jnp.float32
    )
    return hidden.astype(jnp.bfloat16)


def solution(mesh):
    return jax.shard_map(
        per_device,
        mesh=mesh,
        in_specs=(
            P(("grp", "seq"), None),
            P(("grp", "seq")),
            P(("grp", "seq")),
            P(),
            P(),
            P(),
            P(),
            P(),
            P(),
            P(),
            P(),
            P(),
            P(),
            P(),
        ),
        out_specs=P(("grp", "seq"), None),
        check_vma=False,
    )
```

```python
import jax
import jax.numpy as jnp
from jax import lax
from jax.sharding import PartitionSpec as P

E = 1536
HEAD_DIM = 64
NS = 128
KERNEL = 4
HEADS = 24


fast = lax.Precision.HIGH
epsilon = 1e-05


def rms_scale(values, scale_gain):
    mean_sq = jnp.mean(values * values, axis=-1, keepdims=True)
    return values * lax.rsqrt(mean_sq + epsilon) * scale_gain


def route_tiles(tile_embeds, tile_pos, tile_count, devices, rows):
    slots, width = tile_embeds.shape
    capacity = slots // devices
    is_live = jnp.arange(slots, dtype=jnp.int32) < tile_count[0]
    owners = jnp.where(is_live, tile_pos // rows, devices)
    one_hot = (owners[:, None] == jnp.arange(devices, dtype=jnp.int32)[None, :]).astype(jnp.int32)
    ranking = jnp.sum(jnp.cumsum(one_hot, axis=0) * one_hot, axis=1) - 1
    target = jnp.where(is_live, owners * capacity + ranking, -1)
    match = target[None, :] == jnp.arange(devices * capacity, dtype=jnp.int32)[:, None]
    row_column = (tile_pos % rows + 1).astype(jnp.bfloat16)[:, None]
    source = jnp.concatenate(
        [tile_embeds, jnp.pad(row_column, ((0, 0), (0, 127)))], axis=1
    )
    send = jnp.dot(match.astype(jnp.bfloat16), source, preferred_element_type=jnp.float32)
    send = send.astype(jnp.bfloat16).reshape(devices, capacity, width + 128)
    arrived = lax.all_to_all(send, "seq", 0, 0, tiled=True).reshape(devices * capacity, width + 128)
    arrived_rows = arrived[:, width].astype(jnp.float32).astype(jnp.int32) - 1
    place = arrived_rows[None, :] == jnp.arange(rows, dtype=jnp.int32)[:, None]
    tiles = jnp.dot(
        place.astype(jnp.bfloat16), arrived[:, :width], preferred_element_type=jnp.float32
    )
    return tiles.astype(jnp.bfloat16)


def halo(normed, in_weight, width):
    size = lax.axis_size("seq")
    up = [(i, i + 1) for i in range(size - 1)]
    down = [(i + 1, i) for i in range(size - 1)]
    before = lax.ppermute(normed[-width:], "seq", up)
    after = lax.ppermute(normed[:width], "seq", down)
    rows = jnp.concatenate([before, after], axis=0)
    return lax.dot_general(
        in_weight[:, E:], rows, (((0,), (1,)), ((), ())), preferred_element_type=jnp.float32
    ).astype(jnp.bfloat16)


def local_terms(activated, step_size, decay_rate, backward):
    rows = activated.shape[1]
    signal = activated[:E].reshape(HEADS, HEAD_DIM, rows)
    write_map = activated[E : E + NS]
    read_map = activated[E + NS :]
    log_step = step_size * decay_rate[:, None]
    positions = jnp.arange(rows)
    if backward:
        upper = positions[:, None] >= positions[None, :]
    else:
        upper = positions[:, None] <= positions[None, :]
    log_decay = jnp.dot(log_step, upper.astype(jnp.float32), precision=lax.Precision.HIGHEST)
    if backward:
        mask = positions[:, None] <= positions[None, :]
        edge = log_decay[:, :1]
    else:
        mask = positions[:, None] >= positions[None, :]
        edge = log_decay[:, -1:]
    gaps = log_decay[:, :, None] - log_decay[:, None, :]
    weights = jnp.exp(jnp.where(mask[None], gaps, -1e30))
    scores = lax.dot_general(read_map, write_map, (((0,), (0,)), ((), ())), precision=fast)
    mixing = scores[None] * weights * step_size[:, None, :]
    within = lax.dot_general(signal, mixing, (((2,), (2,)), ((0,), (0,))), precision=fast)
    tail_weight = jnp.exp(edge - log_decay) * step_size
    own_state = lax.dot_general(
        signal * tail_weight[:, None, :], write_map, (((2,), (1,)), ((), ())), precision=fast
    )
    return within, own_state, jnp.exp(edge[:, 0]), jnp.exp(log_decay), read_map


def combine(earlier, later):
    return (earlier[0] * later[0], later[0][:, None, None] * earlier[1] + later[1])


def transfer(pair, pairs):
    decay, state = pair
    high = decay.astype(jnp.bfloat16)
    low = (decay - high.astype(jnp.float32)).astype(jnp.bfloat16)
    extra = jnp.stack([high, low])
    extra = jnp.pad(extra, ((0, state.shape[1] - 2), (0, state.shape[2] - decay.shape[0])))
    payload = jnp.concatenate([state.astype(jnp.bfloat16), extra[None]], axis=0)
    got = lax.ppermute(payload, "seq", pairs)
    heads = decay.shape[0]
    got_decay = got[heads, 0, :heads].astype(jnp.float32) + got[heads, 1, :heads].astype(jnp.float32)
    return got_decay, got[:heads].astype(jnp.float32)


def exchange(forward, backward, ties, late, late_input):
    size, me = lax.axis_size("seq"), lax.axis_index("seq")
    chips, chip, is_one = size // 2, me // 2, me % 2 == 1
    swap = [(2 * k + d, 2 * k + 1 - d) for k in range(chips) for d in range(2)]
    pick = lambda a, b: jax.tree.map(lambda x, y: jnp.where(is_one, x, y), a, b)
    mine = pick(forward, backward)
    first = transfer(pick(backward, forward), swap)
    ties = list(ties)
    if late is not None:
        first_state, late_input = lax.optimization_barrier((first[1], late_input))
        first = (first[0], first_state)
        ties[1] = (late(late_input), ties[1])
    run = combine(first, mine)
    done = (jnp.ones_like(mine[0]), jnp.zeros_like(mine[1]))
    shift, level, tied = 1, 0, []
    while shift < chips:
        if level < len(ties) and ties[level] is not None:
            run, held = lax.optimization_barrier((run, ties[level]))
            tied.append(held)
        level += 1
        pairs = [(2 * k + 1, 2 * (k + shift) + 1) for k in range(chips - shift)]
        pairs += [(2 * (k + shift), 2 * k) for k in range(chips - shift)]
        valid = jnp.where(is_one, chip >= shift, chip + shift < chips)
        got_decay, got_state = transfer(run, pairs)
        got = (jnp.where(valid, got_decay, 1.0), got_state)
        done = combine(got, done)
        if 2 * shift < chips:
            run = combine(got, run)
        shift *= 2
    other = lax.ppermute(done[1].astype(jnp.bfloat16), "seq", swap).astype(jnp.float32)
    mine_in = first[0][:, None, None] * done[1] + first[1]
    return jnp.where(is_one, mine_in, other), jnp.where(is_one, other, mine_in), tied


def per_device(
    tile_embeds,
    tile_pos,
    tile_count,
    slide_weight,
    slide_bias,
    norm_gain,
    in_weight,
    dt_weight,
    conv_weight,
    conv_bias,
    dt_bias,
    a_log,
    out_gain,
    out_weight,
):
    devices = lax.axis_size("seq")
    rows = tile_embeds.shape[0] // 2
    tiles = route_tiles(tile_embeds, tile_pos, tile_count, devices, rows)
    embedded = (
        jnp.dot(tiles, slide_weight, preferred_element_type=jnp.float32) + slide_bias
    ).astype(jnp.bfloat16)
    normed = rms_scale(embedded.astype(jnp.float32), norm_gain).astype(jnp.bfloat16)
    turned = (((0,), (1,)), ((), ()))
    conv_input = lax.dot_general(
        in_weight[:, E:], normed, turned, preferred_element_type=jnp.float32
    ).astype(jnp.bfloat16)
    dt_raw = lax.dot_general(dt_weight, normed, turned, preferred_element_type=jnp.float32)
    def gate_of(values):
        gate_part = lax.dot_general(
            in_weight[:, :E], values, turned, preferred_element_type=jnp.float32
        ).astype(jnp.bfloat16).astype(jnp.float32)
        return jax.nn.silu(gate_part)

    sides = halo(normed, in_weight, KERNEL - 1)
    padded = jnp.concatenate(
        [sides[:, : KERNEL - 1], conv_input, sides[:, KERNEL - 1 :]], axis=1
    ).astype(jnp.float32)
    parts = []
    for direction in range(2):
        summed = conv_bias[direction][:, None] + jnp.zeros((conv_input.shape[0], rows), jnp.float32)
        for offset in range(KERNEL):
            first = offset if direction == 0 else 2 * (KERNEL - 1) - offset
            summed = summed + conv_weight[direction, offset][:, None] * padded[:, first : first + rows]
        activated = jax.nn.silu(summed)
        step_size = jax.nn.softplus(dt_raw + dt_bias[direction][:, None])
        decay_rate = -jnp.exp(a_log[direction])
        parts.append(local_terms(activated, step_size, decay_rate, direction == 1))
    half = HEADS // 2
    low_f, low_b, tied = exchange(
        (parts[0][2][:half], parts[0][1][:half]),
        (parts[1][2][:half], parts[1][1][:half]),
        [None, parts[0][0], parts[1][0]],
        gate_of,
        normed,
    )
    high_f, high_b, _ = exchange(
        (parts[0][2][half:], parts[0][1][half:]),
        (parts[1][2][half:], parts[1][1][half:]),
        [],
        None,
        None,
    )
    fwd_in = jnp.concatenate([low_f, high_f], axis=0)
    bwd_in = jnp.concatenate([low_b, high_b], axis=0)
    if len(tied) == 2:
        (gate_silu, within_fwd), within_bwd = tied
    else:
        within_fwd, within_bwd, gate_silu = parts[0][0], parts[1][0], gate_of(normed)
    incomings = (fwd_in, bwd_in)
    withins = (within_fwd, within_bwd)
    total = jnp.zeros((HEADS, HEAD_DIM, rows), jnp.float32)
    for direction in range(2):
        _, own_state, device_decay, decay_to, read_map = parts[direction]
        within = withins[direction]
        incoming = incomings[direction]
        carried = lax.dot_general(
            incoming, read_map, (((2,), (0,)), ((), ())), precision=fast
        ) * decay_to[:, None, :]
        total = total + within + carried
    gated = total.reshape(E, rows) * gate_silu
    mean_sq = jnp.mean(gated * gated, axis=0, keepdims=True)
    mixed = (gated * lax.rsqrt(mean_sq + epsilon) * out_gain[:, None]).astype(jnp.bfloat16)
    hidden = embedded.astype(jnp.float32) + lax.dot_general(
        mixed, out_weight, (((0,), (0,)), ((), ())), preferred_element_type=jnp.float32
    )
    return hidden.astype(jnp.bfloat16)


def solution(mesh):
    return jax.shard_map(
        per_device,
        mesh=mesh,
        in_specs=(
            P(("grp", "seq"), None),
            P(("grp", "seq")),
            P(("grp", "seq")),
            P(),
            P(),
            P(),
            P(),
            P(),
            P(),
            P(),
            P(),
            P(),
            P(),
            P(),
        ),
        out_specs=P(("grp", "seq"), None),
        check_vma=False,
    )
```

```python
import jax
import jax.numpy as jnp
from jax import lax
from jax.sharding import PartitionSpec as P

E = 1536
HEAD_DIM = 64
NS = 128
KERNEL = 4
HEADS = 24


fast = lax.Precision.HIGH
epsilon = 1e-05


def rms_scale(values, scale_gain):
    mean_sq = jnp.mean(values * values, axis=-1, keepdims=True)
    return values * lax.rsqrt(mean_sq + epsilon) * scale_gain


def route_tiles(tile_embeds, tile_pos, tile_count, devices, rows):
    slots, width = tile_embeds.shape
    capacity = slots // devices
    is_live = jnp.arange(slots, dtype=jnp.int32) < tile_count[0]
    owners = jnp.where(is_live, tile_pos // rows, devices)
    one_hot = (owners[:, None] == jnp.arange(devices, dtype=jnp.int32)[None, :]).astype(jnp.int32)
    ranking = jnp.sum(jnp.cumsum(one_hot, axis=0) * one_hot, axis=1) - 1
    target = jnp.where(is_live, owners * capacity + ranking, devices * capacity)
    picked = jnp.full((devices * capacity,), slots, jnp.int32)
    picked = picked.at[target].set(jnp.arange(slots, dtype=jnp.int32), mode="drop")
    row_column = (tile_pos % rows + 1).astype(jnp.bfloat16)[:, None]
    source = jnp.concatenate(
        [tile_embeds, jnp.pad(row_column, ((0, 0), (0, 127)))], axis=1
    )
    send = jnp.take(source, picked, axis=0, mode="fill", fill_value=0)
    send = send.reshape(devices, capacity, width + 128)
    arrived = lax.all_to_all(send, "seq", 0, 0, tiled=True).reshape(devices * capacity, width + 128)
    arrived_rows = arrived[:, width].astype(jnp.float32).astype(jnp.int32) - 1
    spots = jnp.where(arrived_rows >= 0, arrived_rows, rows)
    placed = jnp.zeros((rows,), jnp.int32)
    placed = placed.at[spots].set(jnp.arange(devices * capacity, dtype=jnp.int32), mode="drop")
    return jnp.take(arrived[:, :width], placed, axis=0, mode="clip")


def halo(normed, in_weight, width):
    size = lax.axis_size("seq")
    up = [(i, i + 1) for i in range(size - 1)]
    down = [(i + 1, i) for i in range(size - 1)]
    before = lax.ppermute(normed[-width:], "seq", up)
    after = lax.ppermute(normed[:width], "seq", down)
    rows = jnp.concatenate([before, after], axis=0)
    return lax.dot_general(
        in_weight[:, E:], rows, (((0,), (1,)), ((), ())), preferred_element_type=jnp.float32
    ).astype(jnp.bfloat16)


def local_terms(activated, step_size, decay_rate, backward):
    rows = activated.shape[1]
    signal = activated[:E].reshape(HEADS, HEAD_DIM, rows)
    write_map = activated[E : E + NS]
    read_map = activated[E + NS :]
    log_step = step_size * decay_rate[:, None]
    positions = jnp.arange(rows)
    if backward:
        upper = positions[:, None] >= positions[None, :]
    else:
        upper = positions[:, None] <= positions[None, :]
    log_decay = jnp.dot(log_step, upper.astype(jnp.float32), precision=lax.Precision.HIGHEST)
    if backward:
        mask = positions[:, None] <= positions[None, :]
        edge = log_decay[:, :1]
    else:
        mask = positions[:, None] >= positions[None, :]
        edge = log_decay[:, -1:]
    gaps = log_decay[:, :, None] - log_decay[:, None, :]
    weights = jnp.exp(jnp.where(mask[None], gaps, -1e30))
    scores = lax.dot_general(read_map, write_map, (((0,), (0,)), ((), ())), precision=fast)
    mixing = scores[None] * weights * step_size[:, None, :]
    within = lax.dot_general(signal, mixing, (((2,), (2,)), ((0,), (0,))), precision=fast)
    tail_weight = jnp.exp(edge - log_decay) * step_size
    own_state = lax.dot_general(
        signal * tail_weight[:, None, :], write_map, (((2,), (1,)), ((), ())), precision=fast
    )
    return within, own_state, jnp.exp(edge[:, 0]), jnp.exp(log_decay), read_map


def combine(earlier, later):
    return (earlier[0] * later[0], later[0][:, None, None] * earlier[1] + later[1])


def transfer(pair, pairs):
    decay, state = pair
    high = decay.astype(jnp.bfloat16)
    low = (decay - high.astype(jnp.float32)).astype(jnp.bfloat16)
    extra = jnp.stack([high, low])
    extra = jnp.pad(extra, ((0, state.shape[1] - 2), (0, state.shape[2] - decay.shape[0])))
    payload = jnp.concatenate([state.astype(jnp.bfloat16), extra[None]], axis=0)
    got = lax.ppermute(payload, "seq", pairs)
    heads = decay.shape[0]
    got_decay = got[heads, 0, :heads].astype(jnp.float32) + got[heads, 1, :heads].astype(jnp.float32)
    return got_decay, got[:heads].astype(jnp.float32)


def exchange(forward, backward, ties):
    size, me = lax.axis_size("seq"), lax.axis_index("seq")
    chips, chip, is_one = size // 2, me // 2, me % 2 == 1
    swap = [(2 * k + d, 2 * k + 1 - d) for k in range(chips) for d in range(2)]
    pick = lambda a, b: jax.tree.map(lambda x, y: jnp.where(is_one, x, y), a, b)
    mine = pick(forward, backward)
    first = transfer(pick(backward, forward), swap)
    run = combine(first, mine)
    done = (jnp.ones_like(mine[0]), jnp.zeros_like(mine[1]))
    shift, level, tied = 1, 0, []
    while shift < chips:
        if level < len(ties) and ties[level] is not None:
            run, held = lax.optimization_barrier((run, ties[level]))
            tied.append(held)
        level += 1
        pairs = [(2 * k + 1, 2 * (k + shift) + 1) for k in range(chips - shift)]
        pairs += [(2 * (k + shift), 2 * k) for k in range(chips - shift)]
        valid = jnp.where(is_one, chip >= shift, chip + shift < chips)
        got_decay, got_state = transfer(run, pairs)
        got = (jnp.where(valid, got_decay, 1.0), got_state)
        done = combine(got, done)
        if 2 * shift < chips:
            run = combine(got, run)
        shift *= 2
    other = lax.ppermute(done[1].astype(jnp.bfloat16), "seq", swap).astype(jnp.float32)
    mine_in = first[0][:, None, None] * done[1] + first[1]
    return jnp.where(is_one, mine_in, other), jnp.where(is_one, other, mine_in), tied


def per_device(
    tile_embeds,
    tile_pos,
    tile_count,
    slide_weight,
    slide_bias,
    norm_gain,
    in_weight,
    dt_weight,
    conv_weight,
    conv_bias,
    dt_bias,
    a_log,
    out_gain,
    out_weight,
):
    devices = lax.axis_size("seq")
    rows = tile_embeds.shape[0] // 2
    tiles = route_tiles(tile_embeds, tile_pos, tile_count, devices, rows)
    embedded = (
        jnp.dot(tiles, slide_weight, preferred_element_type=jnp.float32) + slide_bias
    ).astype(jnp.bfloat16)
    normed = rms_scale(embedded.astype(jnp.float32), norm_gain).astype(jnp.bfloat16)
    turned = (((0,), (1,)), ((), ()))
    conv_input = lax.dot_general(
        in_weight[:, E:], normed, turned, preferred_element_type=jnp.float32
    ).astype(jnp.bfloat16)
    dt_raw = lax.dot_general(dt_weight, normed, turned, preferred_element_type=jnp.float32)
    gate_part = lax.dot_general(
        in_weight[:, :E], normed, turned, preferred_element_type=jnp.float32
    ).astype(jnp.bfloat16).astype(jnp.float32)
    gate_silu = jax.nn.silu(gate_part)
    sides = halo(normed, in_weight, KERNEL - 1)
    padded = jnp.concatenate(
        [sides[:, : KERNEL - 1], conv_input, sides[:, KERNEL - 1 :]], axis=1
    ).astype(jnp.float32)
    parts = []
    for direction in range(2):
        summed = conv_bias[direction][:, None] + jnp.zeros((conv_input.shape[0], rows), jnp.float32)
        for offset in range(KERNEL):
            first = offset if direction == 0 else 2 * (KERNEL - 1) - offset
            summed = summed + conv_weight[direction, offset][:, None] * padded[:, first : first + rows]
        activated = jax.nn.silu(summed)
        step_size = jax.nn.softplus(dt_raw + dt_bias[direction][:, None])
        decay_rate = -jnp.exp(a_log[direction])
        parts.append(local_terms(activated, step_size, decay_rate, direction == 1))
    fwd_in, bwd_in, tied = exchange(
        (parts[0][2], parts[0][1]),
        (parts[1][2], parts[1][1]),
        [None, (gate_silu, parts[0][0]), parts[1][0]],
    )
    if len(tied) == 2:
        (gate_silu, within_fwd), within_bwd = tied
    else:
        within_fwd, within_bwd = parts[0][0], parts[1][0]
    incomings = (fwd_in, bwd_in)
    withins = (within_fwd, within_bwd)
    total = jnp.zeros((HEADS, HEAD_DIM, rows), jnp.float32)
    for direction in range(2):
        _, own_state, device_decay, decay_to, read_map = parts[direction]
        within = withins[direction]
        incoming = incomings[direction]
        carried = lax.dot_general(
            incoming, read_map, (((2,), (0,)), ((), ())), precision=fast
        ) * decay_to[:, None, :]
        total = total + within + carried
    gated = total.reshape(E, rows) * gate_silu
    mean_sq = jnp.mean(gated * gated, axis=0, keepdims=True)
    mixed = (gated * lax.rsqrt(mean_sq + epsilon) * out_gain[:, None]).astype(jnp.bfloat16)
    hidden = embedded.astype(jnp.float32) + lax.dot_general(
        mixed, out_weight, (((0,), (0,)), ((), ())), preferred_element_type=jnp.float32
    )
    return hidden.astype(jnp.bfloat16)


def solution(mesh):
    return jax.shard_map(
        per_device,
        mesh=mesh,
        in_specs=(
            P(("grp", "seq"), None),
            P(("grp", "seq")),
            P(("grp", "seq")),
            P(),
            P(),
            P(),
            P(),
            P(),
            P(),
            P(),
            P(),
            P(),
            P(),
            P(),
        ),
        out_specs=P(("grp", "seq"), None),
        check_vma=False,
    )
```

```python
import jax
import jax.numpy as jnp
from jax import lax
from jax.sharding import PartitionSpec as P

E = 1536
HEAD_DIM = 64
NS = 128
KERNEL = 4
HEADS = 24


fast = lax.Precision.HIGH
epsilon = 1e-05


def rms_scale(values, scale_gain):
    mean_sq = jnp.mean(values * values, axis=-1, keepdims=True)
    return values * lax.rsqrt(mean_sq + epsilon) * scale_gain


def route_tiles(tile_embeds, tile_pos, tile_count, devices, rows):
    slots, width = tile_embeds.shape
    capacity = slots // devices
    is_live = jnp.arange(slots, dtype=jnp.int32) < tile_count[0]
    owners = jnp.where(is_live, tile_pos // rows, devices)
    one_hot = (owners[:, None] == jnp.arange(devices, dtype=jnp.int32)[None, :]).astype(jnp.int32)
    ranking = jnp.sum(jnp.cumsum(one_hot, axis=0) * one_hot, axis=1) - 1
    target = jnp.where(is_live, owners * capacity + ranking, -1)
    match = target[None, :] == jnp.arange(devices * capacity, dtype=jnp.int32)[:, None]
    row_column = (tile_pos % rows + 1).astype(jnp.bfloat16)[:, None]
    source = jnp.concatenate(
        [tile_embeds, jnp.pad(row_column, ((0, 0), (0, 127)))], axis=1
    )
    send = jnp.dot(match.astype(jnp.bfloat16), source, preferred_element_type=jnp.float32)
    send = send.astype(jnp.bfloat16).reshape(devices, capacity, width + 128)
    arrived = lax.all_to_all(send, "seq", 0, 0, tiled=True).reshape(devices * capacity, width + 128)
    arrived_rows = arrived[:, width].astype(jnp.float32).astype(jnp.int32) - 1
    place = arrived_rows[None, :] == jnp.arange(rows, dtype=jnp.int32)[:, None]
    tiles = jnp.dot(
        place.astype(jnp.bfloat16), arrived[:, :width], preferred_element_type=jnp.float32
    )
    return tiles.astype(jnp.bfloat16)


def halo(normed, in_weight, width):
    size = lax.axis_size("seq")
    up = [(i, i + 1) for i in range(size - 1)]
    down = [(i + 1, i) for i in range(size - 1)]
    before = lax.ppermute(normed[-width:], "seq", up)
    after = lax.ppermute(normed[:width], "seq", down)
    rows = jnp.concatenate([before, after], axis=0)
    return lax.dot_general(
        in_weight[:, E:], rows, (((0,), (1,)), ((), ())), preferred_element_type=jnp.float32
    ).astype(jnp.bfloat16)


def local_terms(activated, step_size, decay_rate, backward):
    rows = activated.shape[1]
    signal = activated[:E].reshape(HEADS, HEAD_DIM, rows)
    write_map = activated[E : E + NS]
    read_map = activated[E + NS :]
    log_step = step_size * decay_rate[:, None]
    positions = jnp.arange(rows)
    if backward:
        upper = positions[:, None] >= positions[None, :]
    else:
        upper = positions[:, None] <= positions[None, :]
    log_decay = jnp.dot(log_step, upper.astype(jnp.float32), precision=lax.Precision.HIGHEST)
    if backward:
        mask = positions[:, None] <= positions[None, :]
        edge = log_decay[:, :1]
    else:
        mask = positions[:, None] >= positions[None, :]
        edge = log_decay[:, -1:]
    gaps = log_decay[:, :, None] - log_decay[:, None, :]
    weights = jnp.exp(jnp.where(mask[None], gaps, -1e30))
    scores = lax.dot_general(read_map, write_map, (((0,), (0,)), ((), ())), precision=fast)
    mixing = scores[None] * weights * step_size[:, None, :]
    within = lax.dot_general(signal, mixing, (((2,), (2,)), ((0,), (0,))), precision=fast)
    tail_weight = jnp.exp(edge - log_decay) * step_size
    own_state = lax.dot_general(
        signal * tail_weight[:, None, :], write_map, (((2,), (1,)), ((), ())), precision=fast
    )
    return within, own_state, jnp.exp(edge[:, 0]), jnp.exp(log_decay), read_map


def combine(earlier, later):
    return (earlier[0] * later[0], later[0][:, None, None] * earlier[1] + later[1])


def transfer(pair, pairs):
    decay, state = pair
    high = decay.astype(jnp.bfloat16)
    low = (decay - high.astype(jnp.float32)).astype(jnp.bfloat16)
    extra = jnp.stack([high, low])
    extra = jnp.pad(extra, ((0, state.shape[1] - 2), (0, state.shape[2] - decay.shape[0])))
    payload = jnp.concatenate([state.astype(jnp.bfloat16), extra[None]], axis=0)
    got = lax.ppermute(payload, "seq", pairs)
    heads = decay.shape[0]
    got_decay = got[heads, 0, :heads].astype(jnp.float32) + got[heads, 1, :heads].astype(jnp.float32)
    return got_decay, got[:heads].astype(jnp.float32)


def exchange(forward, backward, ties):
    size, me = lax.axis_size("seq"), lax.axis_index("seq")
    chips, chip, is_one = size // 2, me // 2, me % 2 == 1
    swap = [(2 * k + d, 2 * k + 1 - d) for k in range(chips) for d in range(2)]
    pick = lambda a, b: jax.tree.map(lambda x, y: jnp.where(is_one, x, y), a, b)
    mine = pick(forward, backward)
    first = transfer(pick(backward, forward), swap)
    run = combine(first, mine)
    done = (jnp.ones_like(mine[0]), jnp.zeros_like(mine[1]))
    shift, level, tied = 1, 0, []
    while shift < chips:
        if level < len(ties) and ties[level] is not None:
            run, held = lax.optimization_barrier((run, ties[level]))
            tied.append(held)
        level += 1
        pairs = [(2 * k + 1, 2 * (k + shift) + 1) for k in range(chips - shift)]
        pairs += [(2 * (k + shift), 2 * k) for k in range(chips - shift)]
        valid = jnp.where(is_one, chip >= shift, chip + shift < chips)
        got_decay, got_state = transfer(run, pairs)
        got = (jnp.where(valid, got_decay, 1.0), got_state)
        done = combine(got, done)
        if 2 * shift < chips:
            run = combine(got, run)
        shift *= 2
    other = lax.ppermute(done[1].astype(jnp.bfloat16), "seq", swap).astype(jnp.float32)
    mine_in = first[0][:, None, None] * done[1] + first[1]
    return jnp.where(is_one, mine_in, other), jnp.where(is_one, other, mine_in), tied


def per_device(
    tile_embeds,
    tile_pos,
    tile_count,
    slide_weight,
    slide_bias,
    norm_gain,
    in_weight,
    dt_weight,
    conv_weight,
    conv_bias,
    dt_bias,
    a_log,
    out_gain,
    out_weight,
):
    devices = lax.axis_size("seq")
    rows = tile_embeds.shape[0] // 2
    tiles = route_tiles(tile_embeds, tile_pos, tile_count, devices, rows)
    embedded = (
        jnp.dot(tiles, slide_weight, preferred_element_type=jnp.float32) + slide_bias
    ).astype(jnp.bfloat16)
    normed = rms_scale(embedded.astype(jnp.float32), norm_gain).astype(jnp.bfloat16)
    turned = (((0,), (1,)), ((), ()))
    conv_input = lax.dot_general(
        in_weight[:, E:], normed, turned, preferred_element_type=jnp.float32
    ).astype(jnp.bfloat16)
    dt_raw = lax.dot_general(dt_weight, normed, turned, preferred_element_type=jnp.float32)
    gate_part = lax.dot_general(
        in_weight[:, :E], normed, turned, preferred_element_type=jnp.float32
    ).astype(jnp.bfloat16).astype(jnp.float32)
    gate_silu = jax.nn.silu(gate_part)
    sides = halo(normed, in_weight, KERNEL - 1)
    padded = jnp.concatenate(
        [sides[:, : KERNEL - 1], conv_input, sides[:, KERNEL - 1 :]], axis=1
    ).astype(jnp.float32)
    parts = []
    for direction in range(2):
        summed = conv_bias[direction][:, None] + jnp.zeros((conv_input.shape[0], rows), jnp.float32)
        for offset in range(KERNEL):
            first = offset if direction == 0 else 2 * (KERNEL - 1) - offset
            summed = summed + conv_weight[direction, offset][:, None] * padded[:, first : first + rows]
        activated = jax.nn.silu(summed)
        step_size = jax.nn.softplus(dt_raw + dt_bias[direction][:, None])
        decay_rate = -jnp.exp(a_log[direction])
        parts.append(local_terms(activated, step_size, decay_rate, direction == 1))
    fwd_in, bwd_in, tied = exchange(
        (parts[0][2], parts[0][1]),
        (parts[1][2], parts[1][1]),
        [None, (gate_silu, parts[0][0]), parts[1][0]],
    )
    if len(tied) == 2:
        (gate_silu, within_fwd), within_bwd = tied
    else:
        within_fwd, within_bwd = parts[0][0], parts[1][0]
    incomings = (fwd_in, bwd_in)
    withins = (within_fwd, within_bwd)
    total = jnp.zeros((HEADS, HEAD_DIM, rows), jnp.float32)
    for direction in range(2):
        _, own_state, device_decay, decay_to, read_map = parts[direction]
        within = withins[direction]
        incoming = incomings[direction]
        carried = lax.dot_general(
            incoming, read_map, (((2,), (0,)), ((), ())), precision=fast
        ) * decay_to[:, None, :]
        total = total + within + carried
    gated = total.reshape(E, rows) * gate_silu
    mean_sq = jnp.mean(gated * gated, axis=0, keepdims=True)
    mixed = lax.optimization_barrier(
        (gated * lax.rsqrt(mean_sq + epsilon) * out_gain[:, None]).astype(jnp.bfloat16)
    )
    hidden = embedded.astype(jnp.float32) + lax.dot_general(
        mixed, out_weight, (((0,), (0,)), ((), ())), preferred_element_type=jnp.float32
    )
    return hidden.astype(jnp.bfloat16)


def solution(mesh):
    return jax.shard_map(
        per_device,
        mesh=mesh,
        in_specs=(
            P(("grp", "seq"), None),
            P(("grp", "seq")),
            P(("grp", "seq")),
            P(),
            P(),
            P(),
            P(),
            P(),
            P(),
            P(),
            P(),
            P(),
            P(),
            P(),
        ),
        out_specs=P(("grp", "seq"), None),
        check_vma=False,
    )
```

```python
import jax
import jax.numpy as jnp
from jax import lax
from jax.sharding import PartitionSpec as P

E = 1536
HEAD_DIM = 64
NS = 128
KERNEL = 4
HEADS = 24


fast = lax.Precision.HIGH
epsilon = 1e-05


def rms_scale(values, scale_gain):
    mean_sq = jnp.mean(values * values, axis=-1, keepdims=True)
    return values * lax.rsqrt(mean_sq + epsilon) * scale_gain


def route_tiles(tile_embeds, tile_pos, tile_count, devices, rows):
    slots, width = tile_embeds.shape
    capacity = slots // devices
    is_live = jnp.arange(slots, dtype=jnp.int32) < tile_count[0]
    owners = jnp.where(is_live, tile_pos // rows, devices)
    one_hot = (owners[:, None] == jnp.arange(devices, dtype=jnp.int32)[None, :]).astype(jnp.int32)
    ranking = jnp.sum(jnp.cumsum(one_hot, axis=0) * one_hot, axis=1) - 1
    target = jnp.where(is_live, owners * capacity + ranking, -1)
    match = target[None, :] == jnp.arange(devices * capacity, dtype=jnp.int32)[:, None]
    row_column = (tile_pos % rows + 1).astype(jnp.bfloat16)[:, None]
    source = jnp.concatenate(
        [tile_embeds, jnp.pad(row_column, ((0, 0), (0, 127)))], axis=1
    )
    send = jnp.dot(match.astype(jnp.bfloat16), source, preferred_element_type=jnp.float32)
    send = send.astype(jnp.bfloat16).reshape(devices, capacity, width + 128)
    arrived = lax.all_to_all(send, "seq", 0, 0, tiled=True).reshape(devices * capacity, width + 128)
    arrived_rows = arrived[:, width].astype(jnp.float32).astype(jnp.int32) - 1
    place = arrived_rows[None, :] == jnp.arange(rows, dtype=jnp.int32)[:, None]
    tiles = jnp.dot(
        place.astype(jnp.bfloat16), arrived[:, :width], preferred_element_type=jnp.float32
    )
    return tiles.astype(jnp.bfloat16)


def halo(normed, in_weight, width):
    size = lax.axis_size("seq")
    up = [(i, i + 1) for i in range(size - 1)]
    down = [(i + 1, i) for i in range(size - 1)]
    before = lax.ppermute(normed[-width:], "seq", up)
    after = lax.ppermute(normed[:width], "seq", down)
    rows = jnp.concatenate([before, after], axis=0)
    return lax.dot_general(
        in_weight[:, E:], rows, (((0,), (1,)), ((), ())), preferred_element_type=jnp.float32
    ).astype(jnp.bfloat16)


def local_terms(activated, step_size, decay_rate, backward):
    rows = activated.shape[1]
    signal = activated[:E].reshape(HEADS, HEAD_DIM, rows)
    write_map = activated[E : E + NS]
    read_map = activated[E + NS :]
    log_step = step_size * decay_rate[:, None]
    positions = jnp.arange(rows)
    if backward:
        upper = positions[:, None] >= positions[None, :]
    else:
        upper = positions[:, None] <= positions[None, :]
    log_decay = jnp.dot(log_step, upper.astype(jnp.float32), precision=lax.Precision.HIGHEST)
    if backward:
        mask = positions[:, None] <= positions[None, :]
        edge = log_decay[:, :1]
    else:
        mask = positions[:, None] >= positions[None, :]
        edge = log_decay[:, -1:]
    gaps = log_decay[:, :, None] - log_decay[:, None, :]
    weights = jnp.exp(jnp.where(mask[None], gaps, -1e30))
    scores = lax.dot_general(read_map, write_map, (((0,), (0,)), ((), ())), precision=fast)
    mixing = scores[None] * weights * step_size[:, None, :]
    within = lax.dot_general(signal, mixing, (((2,), (2,)), ((0,), (0,))), precision=fast)
    tail_weight = jnp.exp(edge - log_decay) * step_size
    own_state = lax.dot_general(
        signal * tail_weight[:, None, :], write_map, (((2,), (1,)), ((), ())), precision=fast
    )
    return within, own_state, jnp.exp(edge[:, 0]), jnp.exp(log_decay), read_map


def combine(earlier, later):
    return (earlier[0] * later[0], later[0][:, None, None] * earlier[1] + later[1])


def transfer(pair, pairs):
    decay, state = pair
    high = decay.astype(jnp.bfloat16)
    low = (decay - high.astype(jnp.float32)).astype(jnp.bfloat16)
    extra = jnp.stack([high, low])
    extra = jnp.pad(extra, ((0, state.shape[1] - 2), (0, state.shape[2] - decay.shape[0])))
    payload = jnp.concatenate([state.astype(jnp.bfloat16), extra[None]], axis=0)
    got = lax.ppermute(payload, "seq", pairs)
    heads = decay.shape[0]
    got_decay = got[heads, 0, :heads].astype(jnp.float32) + got[heads, 1, :heads].astype(jnp.float32)
    return got_decay, got[:heads].astype(jnp.float32)


def exchange(forward, backward, ties):
    size, me = lax.axis_size("seq"), lax.axis_index("seq")
    chips, chip, is_one = size // 2, me // 2, me % 2 == 1
    swap = [(2 * k + d, 2 * k + 1 - d) for k in range(chips) for d in range(2)]
    pick = lambda a, b: jax.tree.map(lambda x, y: jnp.where(is_one, x, y), a, b)
    mine = pick(forward, backward)
    first = transfer(pick(backward, forward), swap)
    run = combine(first, mine)
    done = (jnp.ones_like(mine[0]), jnp.zeros_like(mine[1]))
    shift, level, tied = 1, 0, []
    while shift < chips:
        if level < len(ties) and ties[level] is not None:
            run, held = lax.optimization_barrier((run, ties[level]))
            tied.append(held)
        level += 1
        pairs = [(2 * k + 1, 2 * (k + shift) + 1) for k in range(chips - shift)]
        pairs += [(2 * (k + shift), 2 * k) for k in range(chips - shift)]
        valid = jnp.where(is_one, chip >= shift, chip + shift < chips)
        got_decay, got_state = transfer(run, pairs)
        got = (jnp.where(valid, got_decay, 1.0), got_state)
        done = combine(got, done)
        if 2 * shift < chips:
            run = combine(got, run)
        shift *= 2
    other = lax.ppermute(done[1].astype(jnp.bfloat16), "seq", swap).astype(jnp.float32)
    mine_in = first[0][:, None, None] * done[1] + first[1]
    return mine_in, other, tied, is_one


def per_device(
    tile_embeds,
    tile_pos,
    tile_count,
    slide_weight,
    slide_bias,
    norm_gain,
    in_weight,
    dt_weight,
    conv_weight,
    conv_bias,
    dt_bias,
    a_log,
    out_gain,
    out_weight,
):
    devices = lax.axis_size("seq")
    rows = tile_embeds.shape[0] // 2
    tiles = route_tiles(tile_embeds, tile_pos, tile_count, devices, rows)
    embedded = (
        jnp.dot(tiles, slide_weight, preferred_element_type=jnp.float32) + slide_bias
    ).astype(jnp.bfloat16)
    normed = rms_scale(embedded.astype(jnp.float32), norm_gain).astype(jnp.bfloat16)
    turned = (((0,), (1,)), ((), ()))
    conv_input = lax.dot_general(
        in_weight[:, E:], normed, turned, preferred_element_type=jnp.float32
    ).astype(jnp.bfloat16)
    dt_raw = lax.dot_general(dt_weight, normed, turned, preferred_element_type=jnp.float32)
    gate_part = lax.dot_general(
        in_weight[:, :E], normed, turned, preferred_element_type=jnp.float32
    ).astype(jnp.bfloat16).astype(jnp.float32)
    gate_silu = jax.nn.silu(gate_part)
    sides = halo(normed, in_weight, KERNEL - 1)
    padded = jnp.concatenate(
        [sides[:, : KERNEL - 1], conv_input, sides[:, KERNEL - 1 :]], axis=1
    ).astype(jnp.float32)
    parts = []
    for direction in range(2):
        summed = conv_bias[direction][:, None] + jnp.zeros((conv_input.shape[0], rows), jnp.float32)
        for offset in range(KERNEL):
            first = offset if direction == 0 else 2 * (KERNEL - 1) - offset
            summed = summed + conv_weight[direction, offset][:, None] * padded[:, first : first + rows]
        activated = jax.nn.silu(summed)
        step_size = jax.nn.softplus(dt_raw + dt_bias[direction][:, None])
        decay_rate = -jnp.exp(a_log[direction])
        parts.append(local_terms(activated, step_size, decay_rate, direction == 1))
    mine_in, other_in, tied, is_one = exchange(
        (parts[0][2], parts[0][1]),
        (parts[1][2], parts[1][1]),
        [None, (gate_silu, parts[0][0]), parts[1][0]],
    )
    if len(tied) == 2:
        (gate_silu, within_fwd), within_bwd = tied
    else:
        within_fwd, within_bwd = parts[0][0], parts[1][0]
    reads = (parts[0][4], parts[1][4])
    decays_to = (parts[0][3], parts[1][3])
    total = within_fwd + within_bwd
    for incoming, first, second in ((mine_in, 0, 1), (other_in, 1, 0)):
        read_map = jnp.where(is_one, reads[first], reads[second])
        decay_to = jnp.where(is_one, decays_to[first], decays_to[second])
        carried = lax.dot_general(
            incoming, read_map, (((2,), (0,)), ((), ())), precision=fast
        ) * decay_to[:, None, :]
        total = total + carried
    gated = total.reshape(E, rows) * gate_silu
    mean_sq = jnp.mean(gated * gated, axis=0, keepdims=True)
    mixed = (gated * lax.rsqrt(mean_sq + epsilon) * out_gain[:, None]).astype(jnp.bfloat16)
    hidden = embedded.astype(jnp.float32) + lax.dot_general(
        mixed, out_weight, (((0,), (0,)), ((), ())), preferred_element_type=jnp.float32
    )
    return hidden.astype(jnp.bfloat16)


def solution(mesh):
    return jax.shard_map(
        per_device,
        mesh=mesh,
        in_specs=(
            P(("grp", "seq"), None),
            P(("grp", "seq")),
            P(("grp", "seq")),
            P(),
            P(),
            P(),
            P(),
            P(),
            P(),
            P(),
            P(),
            P(),
            P(),
            P(),
        ),
        out_specs=P(("grp", "seq"), None),
        check_vma=False,
    )
```

```python
import jax
import jax.numpy as jnp
from jax import lax
from jax.sharding import PartitionSpec as P

E = 1536
HEAD_DIM = 64
NS = 128
KERNEL = 4
HEADS = 24


fast = lax.Precision.HIGH
epsilon = 1e-05


def rms_scale(values, scale_gain):
    mean_sq = jnp.mean(values * values, axis=-1, keepdims=True)
    return values * lax.rsqrt(mean_sq + epsilon) * scale_gain


def route_tiles(tile_embeds, tile_pos, tile_count, devices, rows):
    slots, width = tile_embeds.shape
    capacity = slots // devices
    is_live = jnp.arange(slots, dtype=jnp.int32) < tile_count[0]
    owners = jnp.where(is_live, tile_pos // rows, devices)
    one_hot = (owners[:, None] == jnp.arange(devices, dtype=jnp.int32)[None, :]).astype(jnp.int32)
    ranking = jnp.sum(jnp.cumsum(one_hot, axis=0) * one_hot, axis=1) - 1
    target = jnp.where(is_live, owners * capacity + ranking, -1)
    match = target[None, :] == jnp.arange(devices * capacity, dtype=jnp.int32)[:, None]
    row_column = (tile_pos % rows + 1).astype(jnp.bfloat16)[:, None]
    source = jnp.concatenate(
        [tile_embeds, jnp.pad(row_column, ((0, 0), (0, 127)))], axis=1
    )
    send = jnp.dot(match.astype(jnp.bfloat16), source, preferred_element_type=jnp.float32)
    send = send.astype(jnp.bfloat16).reshape(devices, capacity, width + 128)
    arrived = lax.all_to_all(send, "seq", 0, 0, tiled=True).reshape(devices * capacity, width + 128)
    arrived_rows = arrived[:, width].astype(jnp.float32).astype(jnp.int32) - 1
    place = arrived_rows[None, :] == jnp.arange(rows, dtype=jnp.int32)[:, None]
    tiles = jnp.dot(
        place.astype(jnp.bfloat16), arrived[:, :width], preferred_element_type=jnp.float32
    )
    return tiles.astype(jnp.bfloat16)


def halo(normed, in_weight, width):
    size = lax.axis_size("seq")
    up = [(i, i + 1) for i in range(size - 1)]
    down = [(i + 1, i) for i in range(size - 1)]
    before = lax.ppermute(normed[-width:], "seq", up)
    after = lax.ppermute(normed[:width], "seq", down)
    rows = jnp.concatenate([before, after], axis=0)
    return lax.dot_general(
        in_weight[:, E:], rows, (((0,), (1,)), ((), ())), preferred_element_type=jnp.float32
    ).astype(jnp.bfloat16)


def local_terms(activated, step_size, decay_rate, backward):
    rows = activated.shape[1]
    signal = activated[:E].reshape(HEADS, HEAD_DIM, rows)
    write_map = activated[E : E + NS]
    read_map = activated[E + NS :]
    log_step = step_size * decay_rate[:, None]
    positions = jnp.arange(rows)
    if backward:
        upper = positions[:, None] >= positions[None, :]
    else:
        upper = positions[:, None] <= positions[None, :]
    log_decay = jnp.dot(log_step, upper.astype(jnp.float32), precision=lax.Precision.HIGHEST)
    if backward:
        mask = positions[:, None] <= positions[None, :]
        edge = log_decay[:, :1]
    else:
        mask = positions[:, None] >= positions[None, :]
        edge = log_decay[:, -1:]
    gaps = log_decay[:, :, None] - log_decay[:, None, :]
    weights = jnp.exp(jnp.where(mask[None], gaps, -1e30))
    scores = lax.dot_general(read_map, write_map, (((0,), (0,)), ((), ())), precision=fast)
    mixing = scores[None] * weights * step_size[:, None, :]
    within = lax.dot_general(signal, mixing, (((2,), (2,)), ((0,), (0,))), precision=fast)
    tail_weight = jnp.exp(edge - log_decay) * step_size
    own_state = lax.dot_general(
        signal * tail_weight[:, None, :], write_map, (((2,), (1,)), ((), ())), precision=fast
    )
    return within, own_state, jnp.exp(edge[:, 0]), jnp.exp(log_decay), read_map


def combine(earlier, later):
    return (earlier[0] * later[0], later[0][:, None, None] * earlier[1] + later[1])


def transfer(pair, pairs):
    decay, state = pair
    high = decay.astype(jnp.bfloat16)
    low = (decay - high.astype(jnp.float32)).astype(jnp.bfloat16)
    extra = jnp.stack([high, low])
    extra = jnp.pad(extra, ((0, state.shape[1] - 2), (0, state.shape[2] - decay.shape[0])))
    payload = jnp.concatenate([state.astype(jnp.bfloat16), extra[None]], axis=0)
    got = lax.ppermute(payload, "seq", pairs)
    heads, slab = decay.shape[0], state.shape[0]
    got_decay = got[slab, 0, :heads].astype(jnp.float32) + got[slab, 1, :heads].astype(jnp.float32)
    return got_decay, got[:slab].astype(jnp.float32)


def exchange(forward, backward, ties):
    size, me = lax.axis_size("seq"), lax.axis_index("seq")
    chips, chip, is_one = size // 2, me // 2, me % 2 == 1
    swap = [(2 * k + d, 2 * k + 1 - d) for k in range(chips) for d in range(2)]
    pick = lambda a, b: jax.tree.map(lambda x, y: jnp.where(is_one, x, y), a, b)
    mine = pick(forward, backward)
    first = transfer(pick(backward, forward), swap)
    run = combine(first, mine)
    done = (jnp.ones_like(mine[0]), jnp.zeros_like(mine[1]))
    shift, level, tied = 1, 0, []
    while shift < chips:
        if level < len(ties) and ties[level] is not None:
            run, held = lax.optimization_barrier((run, ties[level]))
            tied.append(held)
        level += 1
        pairs = [(2 * k + 1, 2 * (k + shift) + 1) for k in range(chips - shift)]
        pairs += [(2 * (k + shift), 2 * k) for k in range(chips - shift)]
        valid = jnp.where(is_one, chip >= shift, chip + shift < chips)
        if 2 * shift >= chips and chips - shift == shift:
            half = run[1].shape[0] // 2
            hand = [(2 * k + 1, 2 * k) for k in range(shift)]
            hand += [(2 * k, 2 * k + 1) for k in range(shift, chips)]
            handed = lax.ppermute(run[1][half:].astype(jnp.bfloat16), "seq", hand)
            got_decay, got_low = transfer((run[0], run[1][:half]), pairs)
            relay = [(2 * k, 2 * (k + shift) + 1) for k in range(shift)]
            relay += [(2 * (k + shift) + 1, 2 * k) for k in range(shift)]
            got_high = lax.ppermute(handed, "seq", relay).astype(jnp.float32)
            got_state = jnp.concatenate([got_low, got_high], axis=0)
        else:
            got_decay, got_state = transfer(run, pairs)
        got = (jnp.where(valid, got_decay, 1.0), got_state)
        done = combine(got, done)
        if 2 * shift < chips:
            run = combine(got, run)
        shift *= 2
    other = lax.ppermute(done[1].astype(jnp.bfloat16), "seq", swap).astype(jnp.float32)
    mine_in = first[0][:, None, None] * done[1] + first[1]
    return mine_in, other, tied, is_one


def per_device(
    tile_embeds,
    tile_pos,
    tile_count,
    slide_weight,
    slide_bias,
    norm_gain,
    in_weight,
    dt_weight,
    conv_weight,
    conv_bias,
    dt_bias,
    a_log,
    out_gain,
    out_weight,
):
    devices = lax.axis_size("seq")
    rows = tile_embeds.shape[0] // 2
    tiles = route_tiles(tile_embeds, tile_pos, tile_count, devices, rows)
    embedded = (
        jnp.dot(tiles, slide_weight, preferred_element_type=jnp.float32) + slide_bias
    ).astype(jnp.bfloat16)
    normed = rms_scale(embedded.astype(jnp.float32), norm_gain).astype(jnp.bfloat16)
    turned = (((0,), (1,)), ((), ()))
    conv_input = lax.dot_general(
        in_weight[:, E:], normed, turned, preferred_element_type=jnp.float32
    ).astype(jnp.bfloat16)
    dt_raw = lax.dot_general(dt_weight, normed, turned, preferred_element_type=jnp.float32)
    gate_part = lax.dot_general(
        in_weight[:, :E], normed, turned, preferred_element_type=jnp.float32
    ).astype(jnp.bfloat16).astype(jnp.float32)
    gate_silu = jax.nn.silu(gate_part)
    sides = halo(normed, in_weight, KERNEL - 1)
    padded = jnp.concatenate(
        [sides[:, : KERNEL - 1], conv_input, sides[:, KERNEL - 1 :]], axis=1
    ).astype(jnp.float32)
    parts = []
    for direction in range(2):
        summed = conv_bias[direction][:, None] + jnp.zeros((conv_input.shape[0], rows), jnp.float32)
        for offset in range(KERNEL):
            first = offset if direction == 0 else 2 * (KERNEL - 1) - offset
            summed = summed + conv_weight[direction, offset][:, None] * padded[:, first : first + rows]
        activated = jax.nn.silu(summed)
        step_size = jax.nn.softplus(dt_raw + dt_bias[direction][:, None])
        decay_rate = -jnp.exp(a_log[direction])
        parts.append(local_terms(activated, step_size, decay_rate, direction == 1))
    mine_in, other_in, tied, is_one = exchange(
        (parts[0][2], parts[0][1]),
        (parts[1][2], parts[1][1]),
        [None, (gate_silu, parts[0][0]), parts[1][0]],
    )
    if len(tied) == 2:
        (gate_silu, within_fwd), within_bwd = tied
    else:
        within_fwd, within_bwd = parts[0][0], parts[1][0]
    reads = (parts[0][4], parts[1][4])
    decays_to = (parts[0][3], parts[1][3])
    total = within_fwd + within_bwd
    for incoming, first, second in ((mine_in, 0, 1), (other_in, 1, 0)):
        read_map = jnp.where(is_one, reads[first], reads[second])
        decay_to = jnp.where(is_one, decays_to[first], decays_to[second])
        carried = lax.dot_general(
            incoming, read_map, (((2,), (0,)), ((), ())), precision=fast
        ) * decay_to[:, None, :]
        total = total + carried
    gated = total.reshape(E, rows) * gate_silu
    mean_sq = jnp.mean(gated * gated, axis=0, keepdims=True)
    mixed = (gated * lax.rsqrt(mean_sq + epsilon) * out_gain[:, None]).astype(jnp.bfloat16)
    hidden = embedded.astype(jnp.float32) + lax.dot_general(
        mixed, out_weight, (((0,), (0,)), ((), ())), preferred_element_type=jnp.float32
    )
    return hidden.astype(jnp.bfloat16)


def solution(mesh):
    return jax.shard_map(
        per_device,
        mesh=mesh,
        in_specs=(
            P(("grp", "seq"), None),
            P(("grp", "seq")),
            P(("grp", "seq")),
            P(),
            P(),
            P(),
            P(),
            P(),
            P(),
            P(),
            P(),
            P(),
            P(),
            P(),
        ),
        out_specs=P(("grp", "seq"), None),
        check_vma=False,
    )
```

```python
import jax
import jax.numpy as jnp
from jax import lax
from jax.sharding import PartitionSpec as P

E = 1536
HEAD_DIM = 64
NS = 128
KERNEL = 4
HEADS = 24


fast = lax.Precision.HIGH
epsilon = 1e-05


def rms_scale(values, scale_gain):
    mean_sq = jnp.mean(values * values, axis=-1, keepdims=True)
    return values * lax.rsqrt(mean_sq + epsilon) * scale_gain


def route_tiles(tile_embeds, tile_pos, tile_count, devices, rows):
    slots, width = tile_embeds.shape
    capacity = slots // devices
    is_live = jnp.arange(slots, dtype=jnp.int32) < tile_count[0]
    owners = jnp.where(is_live, tile_pos // rows, devices)
    one_hot = (owners[:, None] == jnp.arange(devices, dtype=jnp.int32)[None, :]).astype(jnp.bfloat16)
    slot_ids = jnp.arange(slots, dtype=jnp.int32)
    before = (slot_ids[None, :] <= slot_ids[:, None]).astype(jnp.bfloat16)
    counts = jnp.dot(before, one_hot, preferred_element_type=jnp.float32)
    ranking = jnp.sum(counts * one_hot.astype(jnp.float32), axis=1).astype(jnp.int32) - 1
    target = jnp.where(is_live, owners * capacity + ranking, -1)
    match = target[None, :] == jnp.arange(devices * capacity, dtype=jnp.int32)[:, None]
    row_column = (tile_pos % rows + 1).astype(jnp.bfloat16)[:, None]
    source = jnp.concatenate(
        [tile_embeds, jnp.pad(row_column, ((0, 0), (0, 127)))], axis=1
    )
    send = jnp.dot(match.astype(jnp.bfloat16), source, preferred_element_type=jnp.float32)
    send = send.astype(jnp.bfloat16).reshape(devices, capacity, width + 128)
    arrived = lax.all_to_all(send, "seq", 0, 0, tiled=True).reshape(devices * capacity, width + 128)
    arrived_rows = arrived[:, width].astype(jnp.float32).astype(jnp.int32) - 1
    place = arrived_rows[None, :] == jnp.arange(rows, dtype=jnp.int32)[:, None]
    tiles = jnp.dot(
        place.astype(jnp.bfloat16), arrived[:, :width], preferred_element_type=jnp.float32
    )
    return tiles.astype(jnp.bfloat16)


def halo(normed, in_weight, width):
    size = lax.axis_size("seq")
    up = [(i, i + 1) for i in range(size - 1)]
    down = [(i + 1, i) for i in range(size - 1)]
    before = lax.ppermute(normed[-width:], "seq", up)
    after = lax.ppermute(normed[:width], "seq", down)
    rows = jnp.concatenate([before, after], axis=0)
    return lax.dot_general(
        in_weight[:, E:], rows, (((0,), (1,)), ((), ())), preferred_element_type=jnp.float32
    ).astype(jnp.bfloat16)


def local_terms(activated, step_size, decay_rate, backward):
    rows = activated.shape[1]
    signal = activated[:E].reshape(HEADS, HEAD_DIM, rows)
    write_map = activated[E : E + NS]
    read_map = activated[E + NS :]
    log_step = step_size * decay_rate[:, None]
    positions = jnp.arange(rows)
    if backward:
        upper = positions[:, None] >= positions[None, :]
    else:
        upper = positions[:, None] <= positions[None, :]
    log_decay = jnp.dot(log_step, upper.astype(jnp.float32), precision=lax.Precision.HIGHEST)
    if backward:
        mask = positions[:, None] <= positions[None, :]
        edge = log_decay[:, :1]
    else:
        mask = positions[:, None] >= positions[None, :]
        edge = log_decay[:, -1:]
    gaps = log_decay[:, :, None] - log_decay[:, None, :]
    weights = jnp.exp(jnp.where(mask[None], gaps, -1e30))
    scores = lax.dot_general(read_map, write_map, (((0,), (0,)), ((), ())), precision=fast)
    mixing = scores[None] * weights * step_size[:, None, :]
    within = lax.dot_general(signal, mixing, (((2,), (2,)), ((0,), (0,))), precision=fast)
    tail_weight = jnp.exp(edge - log_decay) * step_size
    own_state = lax.dot_general(
        signal * tail_weight[:, None, :], write_map, (((2,), (1,)), ((), ())), precision=fast
    )
    return within, own_state, jnp.exp(edge[:, 0]), jnp.exp(log_decay), read_map


def combine(earlier, later):
    return (earlier[0] * later[0], later[0][:, None, None] * earlier[1] + later[1])


def transfer(pair, pairs):
    decay, state = pair
    high = decay.astype(jnp.bfloat16)
    low = (decay - high.astype(jnp.float32)).astype(jnp.bfloat16)
    extra = jnp.stack([high, low])
    extra = jnp.pad(extra, ((0, state.shape[1] - 2), (0, state.shape[2] - decay.shape[0])))
    payload = jnp.concatenate([state.astype(jnp.bfloat16), extra[None]], axis=0)
    got = lax.ppermute(payload, "seq", pairs)
    heads = decay.shape[0]
    got_decay = got[heads, 0, :heads].astype(jnp.float32) + got[heads, 1, :heads].astype(jnp.float32)
    return got_decay, got[:heads].astype(jnp.float32)


def exchange(forward, backward, ties):
    size, me = lax.axis_size("seq"), lax.axis_index("seq")
    chips, chip, is_one = size // 2, me // 2, me % 2 == 1
    swap = [(2 * k + d, 2 * k + 1 - d) for k in range(chips) for d in range(2)]
    pick = lambda a, b: jax.tree.map(lambda x, y: jnp.where(is_one, x, y), a, b)
    mine = pick(forward, backward)
    first = transfer(pick(backward, forward), swap)
    run = combine(first, mine)
    done = (jnp.ones_like(mine[0]), jnp.zeros_like(mine[1]))
    shift, level, tied = 1, 0, []
    while shift < chips:
        if level < len(ties) and ties[level] is not None:
            run, held = lax.optimization_barrier((run, ties[level]))
            tied.append(held)
        level += 1
        pairs = [(2 * k + 1, 2 * (k + shift) + 1) for k in range(chips - shift)]
        pairs += [(2 * (k + shift), 2 * k) for k in range(chips - shift)]
        valid = jnp.where(is_one, chip >= shift, chip + shift < chips)
        got_decay, got_state = transfer(run, pairs)
        got = (jnp.where(valid, got_decay, 1.0), got_state)
        done = combine(got, done)
        if 2 * shift < chips:
            run = combine(got, run)
        shift *= 2
    other = lax.ppermute(done[1].astype(jnp.bfloat16), "seq", swap).astype(jnp.float32)
    mine_in = first[0][:, None, None] * done[1] + first[1]
    return mine_in, other, tied, is_one


def per_device(
    tile_embeds,
    tile_pos,
    tile_count,
    slide_weight,
    slide_bias,
    norm_gain,
    in_weight,
    dt_weight,
    conv_weight,
    conv_bias,
    dt_bias,
    a_log,
    out_gain,
    out_weight,
):
    devices = lax.axis_size("seq")
    rows = tile_embeds.shape[0] // 2
    tiles = route_tiles(tile_embeds, tile_pos, tile_count, devices, rows)
    embedded = (
        jnp.dot(tiles, slide_weight, preferred_element_type=jnp.float32) + slide_bias
    ).astype(jnp.bfloat16)
    normed = rms_scale(embedded.astype(jnp.float32), norm_gain).astype(jnp.bfloat16)
    turned = (((0,), (1,)), ((), ()))
    conv_input = lax.dot_general(
        in_weight[:, E:], normed, turned, preferred_element_type=jnp.float32
    ).astype(jnp.bfloat16)
    dt_raw = lax.dot_general(dt_weight, normed, turned, preferred_element_type=jnp.float32)
    gate_part = lax.dot_general(
        in_weight[:, :E], normed, turned, preferred_element_type=jnp.float32
    ).astype(jnp.bfloat16).astype(jnp.float32)
    gate_silu = jax.nn.silu(gate_part)
    sides = halo(normed, in_weight, KERNEL - 1)
    padded = jnp.concatenate(
        [sides[:, : KERNEL - 1], conv_input, sides[:, KERNEL - 1 :]], axis=1
    ).astype(jnp.float32)
    parts = []
    for direction in range(2):
        summed = conv_bias[direction][:, None] + jnp.zeros((conv_input.shape[0], rows), jnp.float32)
        for offset in range(KERNEL):
            first = offset if direction == 0 else 2 * (KERNEL - 1) - offset
            summed = summed + conv_weight[direction, offset][:, None] * padded[:, first : first + rows]
        activated = jax.nn.silu(summed)
        step_size = jax.nn.softplus(dt_raw + dt_bias[direction][:, None])
        decay_rate = -jnp.exp(a_log[direction])
        parts.append(local_terms(activated, step_size, decay_rate, direction == 1))
    mine_in, other_in, tied, is_one = exchange(
        (parts[0][2], parts[0][1]),
        (parts[1][2], parts[1][1]),
        [None, (gate_silu, parts[0][0]), parts[1][0]],
    )
    if len(tied) == 2:
        (gate_silu, within_fwd), within_bwd = tied
    else:
        within_fwd, within_bwd = parts[0][0], parts[1][0]
    reads = (parts[0][4], parts[1][4])
    decays_to = (parts[0][3], parts[1][3])
    total = within_fwd + within_bwd
    for incoming, first, second in ((mine_in, 0, 1), (other_in, 1, 0)):
        read_map = jnp.where(is_one, reads[first], reads[second])
        decay_to = jnp.where(is_one, decays_to[first], decays_to[second])
        carried = lax.dot_general(
            incoming, read_map, (((2,), (0,)), ((), ())), precision=fast
        ) * decay_to[:, None, :]
        total = total + carried
    gated = total.reshape(E, rows) * gate_silu
    mean_sq = jnp.mean(gated * gated, axis=0, keepdims=True)
    mixed = (gated * lax.rsqrt(mean_sq + epsilon) * out_gain[:, None]).astype(jnp.bfloat16)
    hidden = embedded.astype(jnp.float32) + lax.dot_general(
        mixed, out_weight, (((0,), (0,)), ((), ())), preferred_element_type=jnp.float32
    )
    return hidden.astype(jnp.bfloat16)


def solution(mesh):
    return jax.shard_map(
        per_device,
        mesh=mesh,
        in_specs=(
            P(("grp", "seq"), None),
            P(("grp", "seq")),
            P(("grp", "seq")),
            P(),
            P(),
            P(),
            P(),
            P(),
            P(),
            P(),
            P(),
            P(),
            P(),
            P(),
        ),
        out_specs=P(("grp", "seq"), None),
        check_vma=False,
    )
```

```python
import jax
import jax.numpy as jnp
from jax import lax
from jax.sharding import PartitionSpec as P

E = 1536
HEAD_DIM = 64
NS = 128
KERNEL = 4
HEADS = 24


fast = lax.Precision.HIGH
epsilon = 1e-05


def rms_scale(values, scale_gain):
    mean_sq = jnp.mean(values * values, axis=-1, keepdims=True)
    return values * lax.rsqrt(mean_sq + epsilon) * scale_gain


def route_tiles(tile_embeds, tile_pos, tile_count, devices, rows):
    slots, width = tile_embeds.shape
    capacity = slots // devices
    is_live = jnp.arange(slots, dtype=jnp.int32) < tile_count[0]
    owners = jnp.where(is_live, tile_pos // rows, devices)
    one_hot = (owners[:, None] == jnp.arange(devices, dtype=jnp.int32)[None, :]).astype(jnp.bfloat16)
    slot_ids = jnp.arange(slots, dtype=jnp.int32)
    before = (slot_ids[None, :] <= slot_ids[:, None]).astype(jnp.bfloat16)
    counts = jnp.dot(before, one_hot, preferred_element_type=jnp.float32)
    ranking = jnp.sum(counts * one_hot.astype(jnp.float32), axis=1).astype(jnp.int32) - 1
    target = jnp.where(is_live, owners * capacity + ranking, -1)
    match = target[None, :] == jnp.arange(devices * capacity, dtype=jnp.int32)[:, None]
    row_column = (tile_pos % rows + 1).astype(jnp.bfloat16)[:, None]
    source = jnp.concatenate(
        [tile_embeds, jnp.pad(row_column, ((0, 0), (0, 127)))], axis=1
    )
    picker, source = lax.optimization_barrier((match.astype(jnp.bfloat16), source))
    send = jnp.dot(picker, source, preferred_element_type=jnp.float32)
    send = send.astype(jnp.bfloat16).reshape(devices, capacity, width + 128)
    arrived = lax.all_to_all(send, "seq", 0, 0, tiled=True).reshape(devices * capacity, width + 128)
    arrived_rows = arrived[:, width].astype(jnp.float32).astype(jnp.int32) - 1
    place = arrived_rows[None, :] == jnp.arange(rows, dtype=jnp.int32)[:, None]
    tiles = jnp.dot(
        place.astype(jnp.bfloat16), arrived[:, :width], preferred_element_type=jnp.float32
    )
    return tiles.astype(jnp.bfloat16)


def halo(normed, in_weight, width):
    size = lax.axis_size("seq")
    up = [(i, i + 1) for i in range(size - 1)]
    down = [(i + 1, i) for i in range(size - 1)]
    before = lax.ppermute(normed[-width:], "seq", up)
    after = lax.ppermute(normed[:width], "seq", down)
    rows = jnp.concatenate([before, after], axis=0)
    return lax.dot_general(
        in_weight[:, E:], rows, (((0,), (1,)), ((), ())), preferred_element_type=jnp.float32
    ).astype(jnp.bfloat16)


def local_terms(activated, step_size, decay_rate, backward):
    rows = activated.shape[1]
    signal = activated[:E].reshape(HEADS, HEAD_DIM, rows)
    write_map = activated[E : E + NS]
    read_map = activated[E + NS :]
    log_step = step_size * decay_rate[:, None]
    positions = jnp.arange(rows)
    if backward:
        upper = positions[:, None] >= positions[None, :]
    else:
        upper = positions[:, None] <= positions[None, :]
    log_decay = jnp.dot(log_step, upper.astype(jnp.float32), precision=lax.Precision.HIGHEST)
    if backward:
        mask = positions[:, None] <= positions[None, :]
        edge = log_decay[:, :1]
    else:
        mask = positions[:, None] >= positions[None, :]
        edge = log_decay[:, -1:]
    gaps = log_decay[:, :, None] - log_decay[:, None, :]
    weights = jnp.exp(jnp.where(mask[None], gaps, -1e30))
    scores = lax.dot_general(read_map, write_map, (((0,), (0,)), ((), ())), precision=fast)
    mixing = scores[None] * weights * step_size[:, None, :]
    within = lax.dot_general(signal, mixing, (((2,), (2,)), ((0,), (0,))), precision=fast)
    tail_weight = jnp.exp(edge - log_decay) * step_size
    own_state = lax.dot_general(
        signal * tail_weight[:, None, :], write_map, (((2,), (1,)), ((), ())), precision=fast
    )
    return within, own_state, jnp.exp(edge[:, 0]), jnp.exp(log_decay), read_map


def combine(earlier, later):
    return (earlier[0] * later[0], later[0][:, None, None] * earlier[1] + later[1])


def transfer(pair, pairs):
    decay, state = pair
    high = decay.astype(jnp.bfloat16)
    low = (decay - high.astype(jnp.float32)).astype(jnp.bfloat16)
    extra = jnp.stack([high, low])
    extra = jnp.pad(extra, ((0, state.shape[1] - 2), (0, state.shape[2] - decay.shape[0])))
    payload = jnp.concatenate([state.astype(jnp.bfloat16), extra[None]], axis=0)
    got = lax.ppermute(payload, "seq", pairs)
    heads = decay.shape[0]
    got_decay = got[heads, 0, :heads].astype(jnp.float32) + got[heads, 1, :heads].astype(jnp.float32)
    return got_decay, got[:heads].astype(jnp.float32)


def exchange(forward, backward, ties):
    size, me = lax.axis_size("seq"), lax.axis_index("seq")
    chips, chip, is_one = size // 2, me // 2, me % 2 == 1
    swap = [(2 * k + d, 2 * k + 1 - d) for k in range(chips) for d in range(2)]
    pick = lambda a, b: jax.tree.map(lambda x, y: jnp.where(is_one, x, y), a, b)
    mine = pick(forward, backward)
    first = transfer(pick(backward, forward), swap)
    run = combine(first, mine)
    done = (jnp.ones_like(mine[0]), jnp.zeros_like(mine[1]))
    shift, level, tied = 1, 0, []
    while shift < chips:
        if level < len(ties) and ties[level] is not None:
            run, held = lax.optimization_barrier((run, ties[level]))
            tied.append(held)
        level += 1
        pairs = [(2 * k + 1, 2 * (k + shift) + 1) for k in range(chips - shift)]
        pairs += [(2 * (k + shift), 2 * k) for k in range(chips - shift)]
        valid = jnp.where(is_one, chip >= shift, chip + shift < chips)
        got_decay, got_state = transfer(run, pairs)
        got = (jnp.where(valid, got_decay, 1.0), got_state)
        done = combine(got, done)
        if 2 * shift < chips:
            run = combine(got, run)
        shift *= 2
    other = lax.ppermute(done[1].astype(jnp.bfloat16), "seq", swap).astype(jnp.float32)
    mine_in = first[0][:, None, None] * done[1] + first[1]
    return mine_in, other, tied, is_one


def per_device(
    tile_embeds,
    tile_pos,
    tile_count,
    slide_weight,
    slide_bias,
    norm_gain,
    in_weight,
    dt_weight,
    conv_weight,
    conv_bias,
    dt_bias,
    a_log,
    out_gain,
    out_weight,
):
    devices = lax.axis_size("seq")
    rows = tile_embeds.shape[0] // 2
    tiles = route_tiles(tile_embeds, tile_pos, tile_count, devices, rows)
    embedded = (
        jnp.dot(tiles, slide_weight, preferred_element_type=jnp.float32) + slide_bias
    ).astype(jnp.bfloat16)
    normed = rms_scale(embedded.astype(jnp.float32), norm_gain).astype(jnp.bfloat16)
    turned = (((0,), (1,)), ((), ()))
    conv_input = lax.dot_general(
        in_weight[:, E:], normed, turned, preferred_element_type=jnp.float32
    ).astype(jnp.bfloat16)
    dt_raw = lax.dot_general(dt_weight, normed, turned, preferred_element_type=jnp.float32)
    gate_part = lax.dot_general(
        in_weight[:, :E], normed, turned, preferred_element_type=jnp.float32
    ).astype(jnp.bfloat16).astype(jnp.float32)
    gate_silu = jax.nn.silu(gate_part)
    sides = halo(normed, in_weight, KERNEL - 1)
    padded = jnp.concatenate(
        [sides[:, : KERNEL - 1], conv_input, sides[:, KERNEL - 1 :]], axis=1
    ).astype(jnp.float32)
    parts = []
    for direction in range(2):
        summed = conv_bias[direction][:, None] + jnp.zeros((conv_input.shape[0], rows), jnp.float32)
        for offset in range(KERNEL):
            first = offset if direction == 0 else 2 * (KERNEL - 1) - offset
            summed = summed + conv_weight[direction, offset][:, None] * padded[:, first : first + rows]
        activated = jax.nn.silu(summed)
        step_size = jax.nn.softplus(dt_raw + dt_bias[direction][:, None])
        decay_rate = -jnp.exp(a_log[direction])
        parts.append(local_terms(activated, step_size, decay_rate, direction == 1))
    mine_in, other_in, tied, is_one = exchange(
        (parts[0][2], parts[0][1]),
        (parts[1][2], parts[1][1]),
        [None, (gate_silu, parts[0][0]), parts[1][0]],
    )
    if len(tied) == 2:
        (gate_silu, within_fwd), within_bwd = tied
    else:
        within_fwd, within_bwd = parts[0][0], parts[1][0]
    reads = (parts[0][4], parts[1][4])
    decays_to = (parts[0][3], parts[1][3])
    total = within_fwd + within_bwd
    for incoming, first, second in ((mine_in, 0, 1), (other_in, 1, 0)):
        read_map = jnp.where(is_one, reads[first], reads[second])
        decay_to = jnp.where(is_one, decays_to[first], decays_to[second])
        carried = lax.dot_general(
            incoming, read_map, (((2,), (0,)), ((), ())), precision=fast
        ) * decay_to[:, None, :]
        total = total + carried
    gated = total.reshape(E, rows) * gate_silu
    mean_sq = jnp.mean(gated * gated, axis=0, keepdims=True)
    mixed = (gated * lax.rsqrt(mean_sq + epsilon) * out_gain[:, None]).astype(jnp.bfloat16)
    hidden = embedded.astype(jnp.float32) + lax.dot_general(
        mixed, out_weight, (((0,), (0,)), ((), ())), preferred_element_type=jnp.float32
    )
    return hidden.astype(jnp.bfloat16)


def solution(mesh):
    return jax.shard_map(
        per_device,
        mesh=mesh,
        in_specs=(
            P(("grp", "seq"), None),
            P(("grp", "seq")),
            P(("grp", "seq")),
            P(),
            P(),
            P(),
            P(),
            P(),
            P(),
            P(),
            P(),
            P(),
            P(),
            P(),
        ),
        out_specs=P(("grp", "seq"), None),
        check_vma=False,
    )
```
